512 devices in a mesh: tm: 128 (over y, x, z_lo), batch: 4 (over z_hi, core).
Axes of the slice: x: 4, y: 4, z: 16 (z_hi: 2, z_lo: 8; z = z_hi * 8 + z_lo), core: 2. Of those that a mesh axis runs over, the one named last changes fastest.
Arguments:
- query_states: bfloat16 [4, 16384, 512], P('batch', 'tm'), may hold values from -8 to 8
- key_states: bfloat16 [4, 16384, 512], P('batch', 'tm'), may hold values from -8 to 8
- value_states: bfloat16 [4, 16384, 512], P('batch', 'tm'), may hold values from -6 to 6
- out_proj: bfloat16 [512, 1024], replicated, may hold values from -0.25 to 0.25
- grad_output: bfloat16 [4, 16384, 1024], P('batch', 'tm'), may hold values from -6 to 6
Outputs:
- output: bfloat16 [4, 16384, 1024], P('batch', 'tm')
- grad_query: bfloat16 [4, 16384, 512], P('batch', 'tm')
- grad_key: bfloat16 [4, 16384, 512], P('batch', 'tm')
- grad_value: bfloat16 [4, 16384, 512], P('batch', 'tm')
- grad_proj: float32 [512, 1024], P(('tm', 'batch'))
The draws below stay inside these ranges and needn't reach their ends.
All inputs are finite; a program needn't handle non-finite values.
Results may differ from the reference program's by a relative error of at most 0.02.
Values may be sent and summed in bfloat16 or wider, within the bound.
No kernel may reach another device: no remote copies, remote signals or barrier semaphores. Data moves between devices by JAX's collectives and lax.ppermute only.
A program may use at most 128 MiB of HBM per device.

```python
from functools import partial
import jax
import jax.numpy as jnp
import numpy as np
from jax import lax

D = 1024
HEADS = 8
HD = 64
R2 = 8
R3 = 16
HH = 512
L = 16384
B = 4
SEG1 = 256
SEG2 = 8192


def drawn_pair(key):
    base_q = jnp.clip(jax.random.normal(jax.random.fold_in(key, 11), (B, L, HH), jnp.float32), -6.0, 6.0)
    base_k = jnp.clip(jax.random.normal(jax.random.fold_in(key, 12), (B, L, HH), jnp.float32), -6.0, 6.0)
    return (base_q, base_k)


def draw_query_states(key, part):
    return drawn_pair(key)[0].astype(jnp.bfloat16)


def draw_key_states(key, part):
    return drawn_pair(key)[1].astype(jnp.bfloat16)


def level_of(rng, shape, cuts, low, high):
    def one(dim, shards_of):
        heights = jax.random.uniform(jax.random.fold_in(jax.random.fold_in(rng, 6), dim), (shards_of,), jnp.float32, low / len(cuts), high / len(cuts))
        return jnp.repeat(jnp.exp(heights), shape[dim] // shards_of).reshape((-1,) + (1,) * (len(shape) - dim - 1))

    factor_of = one(*cuts[0])
    for cut in cuts[1:]:
        factor_of = factor_of * one(*cut)
    return factor_of


def gaussian(own_key, extent, scale, bound, cuts=(), kind=jnp.bfloat16):
    entries = scale * jax.random.normal(own_key, extent, jnp.float32)
    if cuts:
        entries = entries * level_of(own_key, extent, cuts, -0.22, 0.18)
    return jnp.clip(entries, -bound, bound).astype(kind)


def setup_inputs(seed: int = 0) -> dict:
    seeds = jax.random.split(jax.random.key(seed), 6)
    query_states = draw_query_states(jax.random.fold_in(seeds[5], 71), 0)
    key_states = draw_key_states(jax.random.fold_in(seeds[5], 71), 0)
    value_states = gaussian(seeds[2], (B, L, HH), 1.0, 6.0, ((0, 4), (1, 128)))
    out_proj = gaussian(seeds[3], (HH, D), HH ** -0.5, 0.25)
    grad_output = gaussian(seeds[4], (B, L, D), 1.0, 6.0, ((0, 4), (1, 128)))
    return dict(query_states=query_states, key_states=key_states, value_states=value_states, out_proj=out_proj, grad_output=grad_output)


def offset_mask(dilation):
    return (np.arange(dilation)[:, None] == (np.arange(HEADS) % dilation)[None, :]).astype(np.float32)


def cover_table(row_count, dilation):
    return (np.arange(row_count) % dilation)[:, None] == (np.arange(HEADS) % dilation)[None, :]


def pick_rows(matrix, dilation):
    count = matrix.shape[0] // dilation
    blocks = matrix.reshape(count, dilation, HEADS, HD)
    chooser = jnp.asarray(offset_mask(dilation), matrix.dtype)[None, :, :, None]
    return jnp.sum(blocks * chooser, axis=1)


def pick_stats(matrix, dilation):
    count = matrix.shape[0] // dilation
    blocks = matrix.reshape(count, dilation, HEADS)
    chooser = jnp.asarray(offset_mask(dilation), matrix.dtype)[None, :, :]
    return jnp.sum(blocks * chooser, axis=1)


def spread_rows(values, dilation):
    chooser = jnp.asarray(offset_mask(dilation), values.dtype)[None, :, :, None]
    return (values[:, None] * chooser).reshape(values.shape[0] * dilation, HEADS, HD)


def spread_stats(values, dilation):
    chooser = jnp.asarray(offset_mask(dilation), values.dtype)[None, :, :]
    return (values[:, None] * chooser).reshape(values.shape[0] * dilation, HEADS)


def merge_levels(log_totals, coverage, partials):
    first_lse = log_totals[0]
    peak = first_lse
    for level_no in range(1, len(log_totals)):
        peak = jnp.maximum(peak, jnp.where(coverage[level_no], log_totals[level_no], first_lse))
    exponents = []
    for level_no in range(len(log_totals)):
        exponents.append(jnp.where(coverage[level_no], jnp.exp(log_totals[level_no] - peak), 0.0))
    denominator = exponents[0]
    for level_no in range(1, len(exponents)):
        denominator = denominator + exponents[level_no]
    weights = []
    merged = None
    for level_no in range(len(exponents)):
        weight_now = exponents[level_no] / denominator
        weights.append(weight_now)
        term = weight_now[:, :, None] * partials[level_no]
        merged = term if merged is None else merged + term
    return merged, weights


def seg_forward(pieces, inv_root):
    queries, keys_now, values_now = pieces
    scores = jnp.einsum("qhd,khd->hqk", queries.astype(jnp.float32), keys_now.astype(jnp.float32)) * inv_root
    peak = jnp.max(scores, axis=2, keepdims=True)
    log_total = peak + jnp.log(jnp.sum(jnp.exp(scores - peak), axis=2, keepdims=True))
    weights_bf = lax.optimization_barrier(jnp.exp(scores - log_total).astype(jnp.bfloat16)).astype(jnp.float32)
    partial_out = jnp.einsum("hqk,khd->qhd", weights_bf, values_now.astype(jnp.float32))
    return partial_out, log_total[:, :, 0].T


def seg_backward(pieces, inv_root):
    queries, keys_now, values_now, grads_now, log_total, offsets = pieces
    q32 = queries.astype(jnp.float32)
    k32 = keys_now.astype(jnp.float32)
    g32 = grads_now.astype(jnp.float32)
    scores = jnp.einsum("qhd,khd->hqk", q32, k32) * inv_root
    prob_full = jnp.exp(scores - log_total.T[:, :, None])
    prob_bf = lax.optimization_barrier(prob_full.astype(jnp.bfloat16)).astype(jnp.float32)
    grad_v = jnp.einsum("hqk,qhd->khd", prob_bf, g32)
    dprob = jnp.einsum("qhd,khd->hqk", g32, values_now.astype(jnp.float32))
    dscore = lax.optimization_barrier((prob_full * (dprob - offsets.T[:, :, None])).astype(jnp.bfloat16)).astype(jnp.float32)
    grad_q = jnp.einsum("hqk,khd->qhd", dscore, k32) * inv_root
    grad_k = jnp.einsum("hqk,qhd->khd", dscore, q32) * inv_root
    return grad_q, grad_k, grad_v


def one_recording(queries, keys_all, values_all, out_proj, upstream):
    inv_root = HD ** -0.5
    level_plan = ((SEG1, 1), (SEG2, R2), (L, R3))
    partials = []
    log_totals = []
    coverage = []
    stored = []
    for segment, dilation in level_plan:
        seg_count = L // segment
        per_seg = segment // dilation
        q_sel = pick_rows(queries, dilation).reshape(seg_count, per_seg, HEADS, HD)
        k_sel = pick_rows(keys_all, dilation).reshape(seg_count, per_seg, HEADS, HD)
        v_sel = pick_rows(values_all, dilation).reshape(seg_count, per_seg, HEADS, HD)
        part_out, seg_lse = lax.map(partial(seg_forward, inv_root=inv_root), (q_sel, k_sel, v_sel))
        partials.append(spread_rows(part_out.reshape(seg_count * per_seg, HEADS, HD), dilation))
        log_totals.append(spread_stats(seg_lse.reshape(seg_count * per_seg, HEADS), dilation))
        coverage.append(cover_table(L, dilation))
        stored.append((q_sel, k_sel, v_sel, seg_lse))
    merged, weights = merge_levels(log_totals, coverage, partials)
    attn = merged.reshape(L, HEADS * HD).astype(jnp.bfloat16)
    output = jnp.dot(attn, out_proj, preferred_element_type=jnp.float32).astype(jnp.bfloat16)
    grad_attn = jnp.dot(upstream, out_proj.T, preferred_element_type=jnp.float32).astype(jnp.bfloat16)
    proj_term = jnp.dot(attn.T, upstream, preferred_element_type=jnp.float32)
    grad_three = grad_attn.astype(jnp.float32).reshape(L, HEADS, HD)
    rowdot = jnp.sum(grad_three * merged, axis=2)
    total_q = jnp.zeros((L, HEADS, HD), jnp.float32)
    total_k = jnp.zeros((L, HEADS, HD), jnp.float32)
    total_v = jnp.zeros((L, HEADS, HD), jnp.float32)
    for level_no in range(3):
        segment, dilation = level_plan[level_no]
        seg_count = L // segment
        per_seg = segment // dilation
        q_sel, k_sel, v_sel, seg_lse = stored[level_no]
        grads_now = (weights[level_no][:, :, None] * grad_three).astype(jnp.bfloat16).reshape(L, HEADS * HD)
        offsets = weights[level_no] * rowdot
        g_sel = pick_rows(grads_now, dilation).reshape(seg_count, per_seg, HEADS, HD)
        c_sel = pick_stats(offsets, dilation).reshape(seg_count, per_seg, HEADS)
        grad_q, grad_k, grad_v = lax.map(partial(seg_backward, inv_root=inv_root), (q_sel, k_sel, v_sel, g_sel, seg_lse, c_sel))
        total_q = total_q + spread_rows(grad_q.reshape(seg_count * per_seg, HEADS, HD), dilation)
        total_k = total_k + spread_rows(grad_k.reshape(seg_count * per_seg, HEADS, HD), dilation)
        total_v = total_v + spread_rows(grad_v.reshape(seg_count * per_seg, HEADS, HD), dilation)
    features = HEADS * HD
    return (output, total_q.reshape(L, features).astype(jnp.bfloat16), total_k.reshape(L, features).astype(jnp.bfloat16), total_v.reshape(L, features).astype(jnp.bfloat16), proj_term)


def reference(query_states, key_states, value_states, out_proj, grad_output):
    outputs = []
    grads_q = []
    grads_k = []
    grads_v = []
    grad_proj = jnp.zeros((HEADS * HD, out_proj.shape[1]), jnp.float32)
    for record in range(B):
        result = one_recording(query_states[record], key_states[record], value_states[record], out_proj, grad_output[record])
        outputs.append(result[0])
        grads_q.append(result[1])
        grads_k.append(result[2])
        grads_v.append(result[3])
        grad_proj = grad_proj + result[4]
    return (jnp.stack(outputs), jnp.stack(grads_q), jnp.stack(grads_k), jnp.stack(grads_v), grad_proj)
```

```python
import jax
import jax.numpy as jnp
import numpy as np
from jax import lax
from jax.sharding import PartitionSpec as P

HEADS = 8
HD = 64
R2 = 8
R3 = 16


def partner(value, axis, apart):
    mask = 2**apart
    pairs = [(source, source ^ mask) for source in range(lax.axis_size(axis))]
    return lax.ppermute(value, axis, pairs)


def offset_mask(dilation):
    return (np.arange(dilation)[:, None] == (np.arange(HEADS) % dilation)[None, :]).astype(
        np.float32
    )


def cover_table(row_count, dilation):
    return (np.arange(row_count) % dilation)[:, None] == (np.arange(HEADS) % dilation)[None, :]


def pick_rows(matrix, dilation):
    count = matrix.shape[0] // dilation
    blocks = matrix.reshape(count, dilation, HEADS, HD)
    chooser = jnp.asarray(offset_mask(dilation), matrix.dtype)[None, :, :, None]
    return jnp.sum(blocks * chooser, axis=1).reshape(count, HEADS * HD)


def pick_stats(matrix, dilation):
    count = matrix.shape[0] // dilation
    blocks = matrix.reshape(count, dilation, HEADS)
    chooser = jnp.asarray(offset_mask(dilation), matrix.dtype)[None, :, :]
    return jnp.sum(blocks * chooser, axis=1)


def spread_rows(values, dilation):
    chooser = jnp.asarray(offset_mask(dilation), values.dtype)[None, :, :, None]
    return (values[:, None] * chooser).reshape(values.shape[0] * dilation, HEADS, HD)


def spread_stats(values, dilation):
    chooser = jnp.asarray(offset_mask(dilation), values.dtype)[None, :, :]
    return (values[:, None] * chooser).reshape(values.shape[0] * dilation, HEADS)


def merge_levels(log_totals, coverage, partials):
    first_lse = log_totals[0]
    peak = first_lse
    for level_no in range(1, len(log_totals)):
        peak = jnp.maximum(peak, jnp.where(coverage[level_no], log_totals[level_no], first_lse))
    exponents = []
    for level_no in range(len(log_totals)):
        exponents.append(jnp.where(coverage[level_no], jnp.exp(log_totals[level_no] - peak), 0.0))
    denominator = exponents[0]
    for level_no in range(1, len(exponents)):
        denominator = denominator + exponents[level_no]
    weights = []
    merged = None
    for level_no in range(len(exponents)):
        weight_now = exponents[level_no] / denominator
        weights.append(weight_now)
        term = weight_now[:, :, None] * partials[level_no]
        merged = term if merged is None else merged + term
    return (merged, weights)


def gather_tm(values, bit_count):
    values = tuple(v[None] for v in values)
    for bit_pos in range(bit_count):
        others = partner(values, "tm", bit_pos)
        values = tuple(jnp.concatenate([mine, theirs], 0) for mine, theirs in zip(values, others))
    return values


def scatter_sum(matrix, axes, bit_order):
    index = lax.axis_index(axes)
    bit_count = len(bit_order)
    size = 1 << bit_count
    block = matrix.reshape((2,) * bit_count + matrix.shape[1:])
    dims = [bit_count - 1 - j for j in range(bit_count)]
    for bit_pos in bit_order:
        axis_pos = dims.index(bit_pos)
        my_bit = index // (1 << bit_pos) % 2
        keep = lax.dynamic_index_in_dim(block, my_bit, axis_pos, keepdims=False)
        send = lax.dynamic_index_in_dim(block, 1 - my_bit, axis_pos, keepdims=False)
        pairs = [(source, source ^ (1 << bit_pos)) for source in range(size)]
        block = keep + lax.ppermute(send, axes, pairs)
        dims.pop(axis_pos)
    return block.reshape((1,) + matrix.shape[1:])


def heads_view(matrix):
    return matrix.reshape(matrix.shape[0], HEADS, HD)


def attend(query_rows, key_rows, value_rows, inv_root):
    scores = (
        jnp.einsum(
            "qhd,khd->hqk",
            heads_view(query_rows),
            heads_view(key_rows),
            preferred_element_type=jnp.float32,
        )
        * inv_root
    )
    peak = jnp.max(scores, axis=2, keepdims=True)
    log_total = peak + jnp.log(jnp.sum(jnp.exp(scores - peak), axis=2, keepdims=True))
    weights_bf = jnp.exp(scores - log_total).astype(jnp.bfloat16)
    part_out = jnp.einsum(
        "hqk,khd->qhd", weights_bf, heads_view(value_rows), preferred_element_type=jnp.float32
    )
    return part_out, log_total[:, :, 0].T


def near_grad(query_rows, key_rows, value_rows, grad_rows, lse_rows, offset_rows, inv_root):
    scores = (
        jnp.einsum(
            "qhd,khd->hqk",
            heads_view(query_rows),
            heads_view(key_rows),
            preferred_element_type=jnp.float32,
        )
        * inv_root
    )
    prob_full = jnp.exp(scores - lse_rows.T[:, :, None])
    dprob = jnp.einsum(
        "qhd,khd->hqk",
        heads_view(grad_rows),
        heads_view(value_rows),
        preferred_element_type=jnp.float32,
    )
    dscore = (prob_full * (dprob - offset_rows.T[:, :, None])).astype(jnp.bfloat16)
    return (
        jnp.einsum("hqk,khd->qhd", dscore, heads_view(key_rows), preferred_element_type=jnp.float32)
        * inv_root
    )


def far_grad(query_group, grad_group, lse_group, offset_group, key_rows, value_rows, inv_root):
    scores_far = (
        jnp.einsum(
            "qhd,khd->hqk",
            heads_view(query_group),
            heads_view(key_rows),
            preferred_element_type=jnp.float32,
        )
        * inv_root
    )
    prob_far = jnp.exp(scores_far - lse_group.T[:, :, None])
    grad_v = jnp.einsum(
        "hqk,qhd->khd",
        prob_far.astype(jnp.bfloat16),
        heads_view(grad_group),
        preferred_element_type=jnp.float32,
    )
    dprob_far = jnp.einsum(
        "qhd,khd->hqk",
        heads_view(grad_group),
        heads_view(value_rows),
        preferred_element_type=jnp.float32,
    )
    dscore_far = (prob_far * (dprob_far - offset_group.T[:, :, None])).astype(jnp.bfloat16)
    grad_k = (
        jnp.einsum(
            "hqk,qhd->khd", dscore_far, heads_view(query_group), preferred_element_type=jnp.float32
        )
        * inv_root
    )
    return grad_k, grad_v


def on_device(query_states, key_states, value_states, out_proj, grad_output):
    queries = query_states[0]
    keys_all = key_states[0]
    values_all = value_states[0]
    upstream = grad_output[0]
    row_count = queries.shape[0]
    features = queries.shape[1]
    inv_root = HD ** (-0.5)
    devices = lax.axis_size("tm")
    bit_count = devices.bit_length() - 1
    half = devices // 2

    other_q, other_k, other_v = partner((queries, keys_all, values_all), "tm", 0)
    keys_one = jnp.concatenate([keys_all, other_k], 0)
    values_one = jnp.concatenate([values_all, other_v], 0)
    part_one, lse_one = attend(queries, keys_one, values_one, inv_root)

    q_two = pick_rows(queries, R2)
    k_two = pick_rows(keys_all, R2)
    v_two = pick_rows(values_all, R2)
    q_all, k_all, v_all = gather_tm((q_two, k_two, v_two), bit_count)
    per_dev = q_two.shape[0]
    k_seg2 = k_all[:half].reshape(half * per_dev, features)
    v_seg2 = v_all[:half].reshape(half * per_dev, features)
    k_seg3 = k_all[:, ::2].reshape(devices * per_dev // 2, features)
    v_seg3 = v_all[:, ::2].reshape(devices * per_dev // 2, features)
    q_three = q_two[::2]
    k_three = k_two[::2]
    v_three = v_two[::2]
    part_two, lse_two = attend(q_two, k_seg2, v_seg2, inv_root)
    part_three, lse_three = attend(q_three, k_seg3, v_seg3, inv_root)

    partials = [spread_rows(part_one, 1), spread_rows(part_two, R2), spread_rows(part_three, R3)]
    log_totals = [spread_stats(lse_one, 1), spread_stats(lse_two, R2), spread_stats(lse_three, R3)]
    coverage = [cover_table(row_count, d) for d in (1, R2, R3)]
    merged, weights = merge_levels(log_totals, coverage, partials)
    attn = merged.reshape(row_count, features).astype(jnp.bfloat16)
    output = jnp.dot(attn, out_proj, preferred_element_type=jnp.float32).astype(jnp.bfloat16)
    grad_attn = lax.dot_general(
        upstream, out_proj, (((1,), (1,)), ((), ())), preferred_element_type=jnp.float32
    ).astype(jnp.bfloat16)
    proj_part = lax.dot_general(
        attn, upstream, (((0,), (0,)), ((), ())), preferred_element_type=jnp.float32
    )
    order = (0, 2, 5, 7, 3, 6, 8, 4, 1)
    grad_proj = scatter_sum(proj_part, ("tm", "batch"), order)

    grad_three = grad_attn.astype(jnp.float32).reshape(row_count, HEADS, HD)
    rowdot = jnp.sum(grad_three * merged, axis=2)

    def grad_of(weight_now, grad_f32):
        return (weight_now[:, :, None] * grad_f32.reshape(-1, HEADS, HD)).astype(jnp.bfloat16)

    grad_one = grad_of(weights[0], grad_three).reshape(row_count, features)
    offset_one = weights[0] * rowdot
    other_g, other_stats = partner(
        (grad_one, jnp.stack([lse_one, offset_one], 0)), "tm", 0
    )
    total_q = spread_rows(
        near_grad(queries, keys_one, values_one, grad_one, lse_one, offset_one, inv_root), 1
    )
    k_g1, v_g1 = far_grad(
        jnp.concatenate([queries, other_q], 0),
        jnp.concatenate([grad_one, other_g], 0),
        jnp.concatenate([lse_one, other_stats[0]], 0),
        jnp.concatenate([offset_one, other_stats[1]], 0),
        keys_all,
        values_all,
        inv_root,
    )
    total_k = spread_rows(k_g1, 1)
    total_v = spread_rows(v_g1, 1)

    ga_two = pick_rows(grad_attn, R2)
    w_two = pick_stats(weights[1], R2)
    w_three = pick_stats(weights[2], R2)
    rd_two = pick_stats(rowdot, R2)
    lse3_rows = pick_stats(spread_stats(lse_three, R3), R2)
    stats = jnp.stack([lse_two, w_two, lse3_rows, w_three, rd_two], 0)
    ga_all, stats_all = gather_tm((ga_two, stats), bit_count)
    ga_all32 = ga_all.astype(jnp.float32)

    g_two = grad_of(w_two, ga_two.astype(jnp.float32)).reshape(per_dev, features)
    c_two = w_two * rd_two
    grad_q2 = near_grad(q_two, k_seg2, v_seg2, g_two, lse_two, c_two, inv_root)
    seg_g2 = grad_of(
        stats_all[:half, 1].reshape(-1, HEADS), ga_all32[:half].reshape(-1, features)
    ).reshape(-1, features)
    seg_c2 = (stats_all[:half, 1] * stats_all[:half, 4]).reshape(-1, HEADS)
    k_g2, v_g2 = far_grad(
        q_all[:half].reshape(-1, features),
        seg_g2,
        stats_all[:half, 0].reshape(-1, HEADS),
        seg_c2,
        k_two,
        v_two,
        inv_root,
    )

    w_three_rows = w_three[::2]
    g_three = grad_of(w_three_rows, ga_two[::2].astype(jnp.float32)).reshape(-1, features)
    c_three = w_three_rows * rd_two[::2]
    grad_q3 = near_grad(q_three, k_seg3, v_seg3, g_three, lse_three, c_three, inv_root)
    seg_w3 = stats_all[:, 3, ::2].reshape(-1, HEADS)
    seg_g3 = grad_of(seg_w3, ga_all32[:, ::2].reshape(-1, features)).reshape(-1, features)
    seg_c3 = seg_w3 * stats_all[:, 4, ::2].reshape(-1, HEADS)
    k_g3, v_g3 = far_grad(
        q_all[:, ::2].reshape(-1, features),
        seg_g3,
        stats_all[:, 2, ::2].reshape(-1, HEADS),
        seg_c3,
        k_three,
        v_three,
        inv_root,
    )

    total_q = total_q + spread_rows(grad_q2, R2) + spread_rows(grad_q3, R3)
    total_k = total_k + spread_rows(k_g2, R2) + spread_rows(k_g3, R3)
    total_v = total_v + spread_rows(v_g2, R2) + spread_rows(v_g3, R3)
    grad_query = total_q.reshape(row_count, features).astype(jnp.bfloat16)
    grad_key = total_k.reshape(row_count, features).astype(jnp.bfloat16)
    grad_value = total_v.reshape(row_count, features).astype(jnp.bfloat16)
    return (output[None], grad_query[None], grad_key[None], grad_value[None], grad_proj)


def solution(mesh):
    in_specs = (
        P("batch", "tm", None),
        P("batch", "tm", None),
        P("batch", "tm", None),
        P(),
        P("batch", "tm", None),
    )
    out_specs = (
        P("batch", "tm", None),
        P("batch", "tm", None),
        P("batch", "tm", None),
        P("batch", "tm", None),
        P(("tm", "batch"), None),
    )
    return jax.shard_map(
        on_device, mesh=mesh, in_specs=in_specs, out_specs=out_specs, check_vma=False
    )
```

```python
import jax
import jax.numpy as jnp
import numpy as np
from jax import lax
from jax.sharding import PartitionSpec as P

HEADS = 8
HD = 64
R2 = 8
R3 = 16


def partner(value, axis, apart):
    mask = 2**apart
    pairs = [(source, source ^ mask) for source in range(lax.axis_size(axis))]
    return lax.ppermute(value, axis, pairs)


def offset_mask(dilation):
    return (np.arange(dilation)[:, None] == (np.arange(HEADS) % dilation)[None, :]).astype(
        np.float32
    )


def cover_table(row_count, dilation):
    return (np.arange(row_count) % dilation)[:, None] == (np.arange(HEADS) % dilation)[None, :]


def pick_rows(matrix, dilation):
    count = matrix.shape[0] // dilation
    blocks = matrix.reshape(count, dilation, HEADS, HD)
    chooser = jnp.asarray(offset_mask(dilation), matrix.dtype)[None, :, :, None]
    return jnp.sum(blocks * chooser, axis=1).reshape(count, HEADS * HD)


def pick_stats(matrix, dilation):
    count = matrix.shape[0] // dilation
    blocks = matrix.reshape(count, dilation, HEADS)
    chooser = jnp.asarray(offset_mask(dilation), matrix.dtype)[None, :, :]
    return jnp.sum(blocks * chooser, axis=1)


def spread_rows(values, dilation):
    chooser = jnp.asarray(offset_mask(dilation), values.dtype)[None, :, :, None]
    return (values[:, None] * chooser).reshape(values.shape[0] * dilation, HEADS, HD)


def spread_stats(values, dilation):
    chooser = jnp.asarray(offset_mask(dilation), values.dtype)[None, :, :]
    return (values[:, None] * chooser).reshape(values.shape[0] * dilation, HEADS)


def merge_levels(log_totals, coverage, partials):
    first_lse = log_totals[0]
    peak = first_lse
    for level_no in range(1, len(log_totals)):
        peak = jnp.maximum(peak, jnp.where(coverage[level_no], log_totals[level_no], first_lse))
    exponents = []
    for level_no in range(len(log_totals)):
        exponents.append(jnp.where(coverage[level_no], jnp.exp(log_totals[level_no] - peak), 0.0))
    denominator = exponents[0]
    for level_no in range(1, len(exponents)):
        denominator = denominator + exponents[level_no]
    weights = []
    merged = None
    for level_no in range(len(exponents)):
        weight_now = exponents[level_no] / denominator
        weights.append(weight_now)
        term = weight_now[:, :, None] * partials[level_no]
        merged = term if merged is None else merged + term
    return (merged, weights)


def gather_blocks(block, axis_pos, bit_order):
    for bit_pos in bit_order:
        block = jnp.concatenate([block, partner(block, "tm", bit_pos)], axis_pos)
    return block


def split_exact(values):
    high = lax.reduce_precision(values, exponent_bits=8, mantissa_bits=7)
    rest = values - high
    middle = lax.reduce_precision(rest, exponent_bits=8, mantissa_bits=7)
    low = rest - middle
    parts = jnp.concatenate([high, middle, low], -1)
    return parts.astype(jnp.bfloat16)


def join_exact(parts):
    width = parts.shape[-1] // 3
    as32 = parts.astype(jnp.float32)
    return as32[..., :width] + (as32[..., width : 2 * width] + as32[..., 2 * width :])


def by_parity(rows):
    return rows.reshape((rows.shape[0] // 2, 2) + rows.shape[1:]).swapaxes(0, 1)


def from_parity(rows):
    return rows.swapaxes(0, 1).reshape((rows.shape[0] * rows.shape[1],) + rows.shape[2:])


def pad_lanes(matrix, width):
    return jnp.pad(matrix, [(0, 0)] * (matrix.ndim - 1) + [(0, width - matrix.shape[-1])])


class HalvingSum:

    def __init__(self, matrix, bit_count):
        self.block = matrix.reshape((2,) * bit_count + matrix.shape[1:])
        self.dims = [bit_count - 1 - j for j in range(bit_count)]
        self.tail = matrix.shape[1:]

    def split(self, bit_pos, my_bit):
        self.axis_pos = self.dims.index(bit_pos)
        self.keep = lax.dynamic_index_in_dim(self.block, my_bit, self.axis_pos, keepdims=False)
        return lax.dynamic_index_in_dim(self.block, 1 - my_bit, self.axis_pos, keepdims=False)

    def absorb(self, received):
        self.block = self.keep + received
        self.dims.pop(self.axis_pos)

    def result(self):
        return self.block.reshape((1,) + self.tail)


def heads_view(matrix):
    return matrix.reshape(matrix.shape[0], HEADS, HD)


def attend(query_rows, key_rows, value_rows, inv_root):
    scores = (
        jnp.einsum(
            "qhd,khd->hqk",
            heads_view(query_rows),
            heads_view(key_rows),
            preferred_element_type=jnp.float32,
        )
        * inv_root
    )
    peak = jnp.max(scores, axis=2, keepdims=True)
    log_total = peak + jnp.log(jnp.sum(jnp.exp(scores - peak), axis=2, keepdims=True))
    weights_bf = jnp.exp(scores - log_total).astype(jnp.bfloat16)
    part_out = jnp.einsum(
        "hqk,khd->qhd", weights_bf, heads_view(value_rows), preferred_element_type=jnp.float32
    )
    return part_out, log_total[:, :, 0].T


def near_grad(query_rows, key_rows, value_rows, grad_rows, lse_rows, offset_rows, inv_root):
    scores = (
        jnp.einsum(
            "qhd,khd->hqk",
            heads_view(query_rows),
            heads_view(key_rows),
            preferred_element_type=jnp.float32,
        )
        * inv_root
    )
    prob_full = jnp.exp(scores - lse_rows.T[:, :, None])
    dprob = jnp.einsum(
        "qhd,khd->hqk",
        heads_view(grad_rows),
        heads_view(value_rows),
        preferred_element_type=jnp.float32,
    )
    dscore = (prob_full * (dprob - offset_rows.T[:, :, None])).astype(jnp.bfloat16)
    return (
        jnp.einsum("hqk,khd->qhd", dscore, heads_view(key_rows), preferred_element_type=jnp.float32)
        * inv_root
    )


def far_grad(query_group, grad_group, lse_group, offset_group, key_rows, value_rows, inv_root):
    scores_far = (
        jnp.einsum(
            "qhd,khd->hqk",
            heads_view(query_group),
            heads_view(key_rows),
            preferred_element_type=jnp.float32,
        )
        * inv_root
    )
    prob_far = jnp.exp(scores_far - lse_group.T[:, :, None])
    grad_v = jnp.einsum(
        "hqk,qhd->khd",
        prob_far.astype(jnp.bfloat16),
        heads_view(grad_group),
        preferred_element_type=jnp.float32,
    )
    dprob_far = jnp.einsum(
        "qhd,khd->hqk",
        heads_view(grad_group),
        heads_view(value_rows),
        preferred_element_type=jnp.float32,
    )
    dscore_far = (prob_far * (dprob_far - offset_group.T[:, :, None])).astype(jnp.bfloat16)
    grad_k = (
        jnp.einsum(
            "hqk,qhd->khd", dscore_far, heads_view(query_group), preferred_element_type=jnp.float32
        )
        * inv_root
    )
    return grad_k, grad_v


def on_device(query_states, key_states, value_states, out_proj, grad_output):
    queries = query_states[0]
    keys_all = key_states[0]
    values_all = value_states[0]
    upstream = grad_output[0]
    row_count = queries.shape[0]
    features = queries.shape[1]
    inv_root = HD ** (-0.5)
    devices = lax.axis_size("tm")
    bit_count = devices.bit_length() - 1
    top_bit = bit_count - 1
    near_first = {0: 0, 1: 2, 2: 1, 3: 4, 4: 3, 5: 5}
    low_bits = sorted(range(top_bit), key=lambda b: near_first.get(b, b))
    tm_index = lax.axis_index("tm")
    batch_index = lax.axis_index("batch")
    batch_count = lax.axis_size("batch")
    batch_bits = batch_count.bit_length() - 1
    wide = features + 128

    qkv = jnp.stack([by_parity(pick_rows(m, R2)) for m in (queries, keys_all, values_all)], 0)
    per_par = qkv.shape[2]
    own = qkv[:, :, None]
    for bit_pos in low_bits:
        if bit_pos == 0:
            other, other_qkv = partner(
                (own, jnp.stack([queries, keys_all, values_all], 0)), "tm", bit_pos
            )
        else:
            other = partner(own, "tm", bit_pos)
        own = jnp.concatenate([own, other], 2)
    far = partner(own[:, 0], "tm", top_bit)
    other_q = other_qkv[0]
    keys_one = jnp.concatenate([keys_all, other_qkv[1]], 0)
    values_one = jnp.concatenate([values_all, other_qkv[2]], 0)
    part_one, lse_one = attend(queries, keys_one, values_one, inv_root)
    q_seg2 = own[0].reshape(-1, features)
    k_seg2 = own[1].reshape(-1, features)
    v_seg2 = own[2].reshape(-1, features)
    q_seg3 = jnp.concatenate([own[0, 0], far[0]], 0).reshape(-1, features)
    k_seg3 = jnp.concatenate([own[1, 0], far[1]], 0).reshape(-1, features)
    v_seg3 = jnp.concatenate([own[2, 0], far[2]], 0).reshape(-1, features)
    q_two = qkv[0].reshape(-1, features)
    q_three = qkv[0, 0]
    part_two, lse_two = attend(q_two, k_seg2, v_seg2, inv_root)
    part_three, lse_three = attend(q_three, k_seg3, v_seg3, inv_root)

    partials = [
        spread_rows(part_one, 1),
        spread_rows(from_parity(part_two.reshape((2, per_par) + part_two.shape[1:])), R2),
        spread_rows(part_three, R3),
    ]
    log_totals = [
        spread_stats(lse_one, 1),
        spread_stats(from_parity(lse_two.reshape(2, per_par, HEADS)), R2),
        spread_stats(lse_three, R3),
    ]
    coverage = [cover_table(row_count, d) for d in (1, R2, R3)]
    merged, weights = merge_levels(log_totals, coverage, partials)
    attn = merged.reshape(row_count, features).astype(jnp.bfloat16)
    output = jnp.dot(attn, out_proj, preferred_element_type=jnp.float32).astype(jnp.bfloat16)
    grad_attn = lax.dot_general(
        upstream, out_proj, (((1,), (1,)), ((), ())), preferred_element_type=jnp.float32
    ).astype(jnp.bfloat16)
    proj_part = lax.dot_general(
        attn, upstream, (((0,), (0,)), ((), ())), preferred_element_type=jnp.float32
    )
    halving = HalvingSum(proj_part, bit_count + batch_bits)

    def batch_step(bit_pos):
        send = halving.split(bit_pos, batch_index // (1 << bit_pos) % 2)
        pairs = [(s, s ^ (1 << bit_pos)) for s in range(batch_count)]
        halving.absorb(lax.ppermute(send, "batch", pairs))

    def tm_send(bit_pos):
        return halving.split(bit_pos + batch_bits, tm_index // (1 << bit_pos) % 2)

    batch_step(0)

    grad_three = grad_attn.astype(jnp.float32).reshape(row_count, HEADS, HD)
    rowdot = jnp.sum(grad_three * merged, axis=2)

    def grad_of(weight_now, grad_rows):
        scaled = weight_now[:, :, None] * grad_rows.astype(jnp.float32).reshape(-1, HEADS, HD)
        return scaled.astype(jnp.bfloat16).reshape(-1, features)

    grad_one = grad_of(weights[0], grad_attn)
    offset_one = weights[0] * rowdot
    packed_one = jnp.concatenate([grad_one, split_exact(jnp.concatenate([lse_one, offset_one], 1))], 1)
    packed_one = pad_lanes(packed_one, wide)

    ga_par = by_parity(pick_rows(grad_attn, R2))
    w_two = by_parity(pick_stats(weights[1], R2))
    rd_two = by_parity(pick_stats(rowdot, R2))
    lse_two_par = lse_two.reshape(2, per_par, HEADS)
    w_three = pick_stats(weights[2], R3)
    no_level = jnp.zeros_like(w_three)
    lse3_par = jnp.stack([lse_three, no_level], 0)
    w3_par = jnp.stack([w_three, no_level], 0)
    stats_par = jnp.concatenate([lse_two_par, w_two, lse3_par, w3_par, rd_two], -1)
    packed = pad_lanes(jnp.concatenate([ga_par, split_exact(stats_par)], -1), wide)
    own_b = packed[:, None]
    for bit_pos in low_bits:
        if bit_pos == 0:
            other, received, other_one = partner(
                (own_b, tm_send(bit_pos), packed_one), "tm", bit_pos
            )
        else:
            other, received = partner((own_b, tm_send(bit_pos)), "tm", bit_pos)
        halving.absorb(received)
        own_b = jnp.concatenate([own_b, other], 1)
    far_b, received = partner((own_b[0], tm_send(top_bit)), "tm", top_bit)
    halving.absorb(received)
    for bit_pos in range(1, batch_bits):
        batch_step(bit_pos)
    grad_proj = halving.result()

    other_stats = join_exact(other_one[:, features : features + 6 * HEADS])
    total_q = spread_rows(
        near_grad(queries, keys_one, values_one, grad_one, lse_one, offset_one, inv_root), 1
    )
    k_g1, v_g1 = far_grad(
        jnp.concatenate([queries, other_q], 0),
        jnp.concatenate([grad_one, other_one[:, :features]], 0),
        jnp.concatenate([lse_one, other_stats[:, :HEADS]], 0),
        jnp.concatenate([offset_one, other_stats[:, HEADS:]], 0),
        keys_all,
        values_all,
        inv_root,
    )
    total_k = spread_rows(k_g1, 1)
    total_v = spread_rows(v_g1, 1)

    stat_w = 5 * HEADS

    def unpack(rows):
        rows = rows.reshape(-1, wide)
        stats = join_exact(rows[:, features : features + 3 * stat_w])
        return rows[:, :features], stats.reshape(-1, 5, HEADS)

    g_two = grad_of(w_two.reshape(-1, HEADS), ga_par.reshape(-1, features))
    c_two = w_two.reshape(-1, HEADS) * rd_two.reshape(-1, HEADS)
    grad_q2 = near_grad(q_two, k_seg2, v_seg2, g_two, lse_two, c_two, inv_root)
    ga_seg2, st_seg2 = unpack(own_b)
    k_g2, v_g2 = far_grad(
        q_seg2,
        grad_of(st_seg2[:, 1], ga_seg2),
        st_seg2[:, 0],
        st_seg2[:, 1] * st_seg2[:, 4],
        qkv[1].reshape(-1, features),
        qkv[2].reshape(-1, features),
        inv_root,
    )

    g_three = grad_of(w_three, ga_par[0])
    c_three = w_three * rd_two[0]
    grad_q3 = near_grad(q_three, k_seg3, v_seg3, g_three, lse_three, c_three, inv_root)
    ga_seg3, st_seg3 = unpack(jnp.concatenate([own_b[0], far_b], 0))
    k_g3, v_g3 = far_grad(
        q_seg3,
        grad_of(st_seg3[:, 3], ga_seg3),
        st_seg3[:, 2],
        st_seg3[:, 3] * st_seg3[:, 4],
        qkv[1, 0],
        qkv[2, 0],
        inv_root,
    )

    def level_two_rows(values):
        return spread_rows(from_parity(values.reshape((2, per_par) + values.shape[1:])), R2)

    total_q = total_q + level_two_rows(grad_q2) + spread_rows(grad_q3, R3)
    total_k = total_k + level_two_rows(k_g2) + spread_rows(k_g3, R3)
    total_v = total_v + level_two_rows(v_g2) + spread_rows(v_g3, R3)
    grad_query = total_q.reshape(row_count, features).astype(jnp.bfloat16)
    grad_key = total_k.reshape(row_count, features).astype(jnp.bfloat16)
    grad_value = total_v.reshape(row_count, features).astype(jnp.bfloat16)
    return (output[None], grad_query[None], grad_key[None], grad_value[None], grad_proj)


def solution(mesh):
    in_specs = (
        P("batch", "tm", None),
        P("batch", "tm", None),
        P("batch", "tm", None),
        P(),
        P("batch", "tm", None),
    )
    out_specs = (
        P("batch", "tm", None),
        P("batch", "tm", None),
        P("batch", "tm", None),
        P("batch", "tm", None),
        P(("tm", "batch"), None),
    )
    return jax.shard_map(
        on_device, mesh=mesh, in_specs=in_specs, out_specs=out_specs, check_vma=False
    )
```

```python
import jax
import jax.numpy as jnp
import numpy as np
from jax import lax
from jax.sharding import PartitionSpec as P

HEADS = 8
HD = 64
R2 = 8
R3 = 16


def partner(value, axis, apart):
    mask = 2**apart
    pairs = [(source, source ^ mask) for source in range(lax.axis_size(axis))]
    return lax.ppermute(value, axis, pairs)


def offset_mask(dilation):
    return (np.arange(dilation)[:, None] == (np.arange(HEADS) % dilation)[None, :]).astype(
        np.float32
    )


def cover_table(row_count, dilation):
    return (np.arange(row_count) % dilation)[:, None] == (np.arange(HEADS) % dilation)[None, :]


def pick_rows(matrix, dilation):
    count = matrix.shape[0] // dilation
    blocks = matrix.reshape(count, dilation, HEADS, HD)
    chooser = jnp.asarray(offset_mask(dilation), matrix.dtype)[None, :, :, None]
    return jnp.sum(blocks * chooser, axis=1).reshape(count, HEADS * HD)


def pick_stats(matrix, dilation):
    count = matrix.shape[0] // dilation
    blocks = matrix.reshape(count, dilation, HEADS)
    chooser = jnp.asarray(offset_mask(dilation), matrix.dtype)[None, :, :]
    return jnp.sum(blocks * chooser, axis=1)


def spread_rows(values, dilation):
    chooser = jnp.asarray(offset_mask(dilation), values.dtype)[None, :, :, None]
    return (values[:, None] * chooser).reshape(values.shape[0] * dilation, HEADS, HD)


def spread_stats(values, dilation):
    chooser = jnp.asarray(offset_mask(dilation), values.dtype)[None, :, :]
    return (values[:, None] * chooser).reshape(values.shape[0] * dilation, HEADS)


def merge_levels(log_totals, coverage, partials):
    first_lse = log_totals[0]
    peak = first_lse
    for level_no in range(1, len(log_totals)):
        peak = jnp.maximum(peak, jnp.where(coverage[level_no], log_totals[level_no], first_lse))
    exponents = []
    for level_no in range(len(log_totals)):
        exponents.append(jnp.where(coverage[level_no], jnp.exp(log_totals[level_no] - peak), 0.0))
    denominator = exponents[0]
    for level_no in range(1, len(exponents)):
        denominator = denominator + exponents[level_no]
    weights = []
    merged = None
    for level_no in range(len(exponents)):
        weight_now = exponents[level_no] / denominator
        weights.append(weight_now)
        term = weight_now[:, :, None] * partials[level_no]
        merged = term if merged is None else merged + term
    return (merged, weights)


def gather_blocks(block, axis_pos, bit_order):
    for bit_pos in bit_order:
        block = jnp.concatenate([block, partner(block, "tm", bit_pos)], axis_pos)
    return block


def split_exact(values):
    high = lax.reduce_precision(values, exponent_bits=8, mantissa_bits=7)
    rest = values - high
    middle = lax.reduce_precision(rest, exponent_bits=8, mantissa_bits=7)
    low = rest - middle
    parts = jnp.concatenate([high, middle, low], -1)
    return parts.astype(jnp.bfloat16)


def join_exact(parts):
    width = parts.shape[-1] // 3
    as32 = parts.astype(jnp.float32)
    return as32[..., :width] + (as32[..., width : 2 * width] + as32[..., 2 * width :])


def by_parity(rows):
    return rows.reshape((rows.shape[0] // 2, 2) + rows.shape[1:]).swapaxes(0, 1)


def from_parity(rows):
    return rows.swapaxes(0, 1).reshape((rows.shape[0] * rows.shape[1],) + rows.shape[2:])


def pad_lanes(matrix, width):
    return jnp.pad(matrix, [(0, 0)] * (matrix.ndim - 1) + [(0, width - matrix.shape[-1])])


def scatter_sum(matrix, axes, bit_order):
    index = lax.axis_index(axes)
    bit_count = len(bit_order)
    size = 1 << bit_count
    block = matrix.reshape((2,) * bit_count + matrix.shape[1:])
    dims = [bit_count - 1 - j for j in range(bit_count)]
    for bit_pos in bit_order:
        axis_pos = dims.index(bit_pos)
        my_bit = index // (1 << bit_pos) % 2
        keep = lax.dynamic_index_in_dim(block, my_bit, axis_pos, keepdims=False)
        send = lax.dynamic_index_in_dim(block, 1 - my_bit, axis_pos, keepdims=False)
        pairs = [(source, source ^ (1 << bit_pos)) for source in range(size)]
        block = keep + lax.ppermute(send, axes, pairs)
        dims.pop(axis_pos)
    return block.reshape((1,) + matrix.shape[1:])


def head_mask():
    return jnp.asarray(np.arange(HEADS)[:, None] == np.arange(HEADS * HD)[None, :] // HD)


def expand_heads(rows):
    mask = head_mask().astype(rows.dtype)
    return (rows[None] * mask[:, None, :]).reshape(HEADS * rows.shape[0], rows.shape[1])


def collapse_heads(rows):
    mask = head_mask().astype(rows.dtype)
    blocks = rows.reshape(HEADS, rows.shape[0] // HEADS, rows.shape[1])
    return jnp.sum(blocks * mask[:, None, :], axis=0).reshape(-1, HEADS, HD)


def dot_nt(left, right):
    return lax.dot_general(left, right, (((1,), (1,)), ((), ())), preferred_element_type=jnp.float32)


def dot_nn(left, right):
    return lax.dot_general(left, right, (((1,), (0,)), ((), ())), preferred_element_type=jnp.float32)


def dot_tn(left, right):
    return lax.dot_general(left, right, (((0,), (0,)), ((), ())), preferred_element_type=jnp.float32)


def per_head_rows(stats):
    return stats.T.reshape(-1, 1)


def attend(query_rows, key_rows, value_rows, inv_root):
    scores = dot_nt(expand_heads(query_rows), key_rows) * inv_root
    peak = jnp.max(scores, axis=1, keepdims=True)
    log_total = peak + jnp.log(jnp.sum(jnp.exp(scores - peak), axis=1, keepdims=True))
    weights_bf = jnp.exp(scores - log_total).astype(jnp.bfloat16)
    part_out = collapse_heads(dot_nn(weights_bf, value_rows))
    return part_out, log_total.reshape(HEADS, -1).T


def near_grad(query_rows, key_rows, value_rows, grad_rows, lse_rows, offset_rows, inv_root):
    scores = dot_nt(expand_heads(query_rows), key_rows) * inv_root
    prob_full = jnp.exp(scores - per_head_rows(lse_rows))
    dprob = dot_nt(expand_heads(grad_rows), value_rows)
    dscore = (prob_full * (dprob - per_head_rows(offset_rows))).astype(jnp.bfloat16)
    return collapse_heads(dot_nn(dscore, key_rows)) * inv_root


def by_head_key(stats, key_count):
    spread = jnp.broadcast_to(stats.T[:, None, :], (HEADS, key_count, stats.shape[0]))
    return spread.reshape(HEADS * key_count, stats.shape[0])


def far_grad(query_group, grad_group, lse_group, offset_group, key_rows, value_rows, inv_root):
    scores_far = dot_nt(expand_heads(key_rows), query_group) * inv_root
    key_count = key_rows.shape[0]
    prob_far = jnp.exp(scores_far - by_head_key(lse_group, key_count))
    grad_v = collapse_heads(dot_nn(prob_far.astype(jnp.bfloat16), grad_group))
    dprob_far = dot_nt(expand_heads(value_rows), grad_group)
    offsets = by_head_key(offset_group, key_count)
    dscore_far = (prob_far * (dprob_far - offsets)).astype(jnp.bfloat16)
    grad_k = collapse_heads(dot_nn(dscore_far, query_group)) * inv_root
    return grad_k, grad_v


def on_device(query_states, key_states, value_states, out_proj, grad_output):
    queries = query_states[0]
    keys_all = key_states[0]
    values_all = value_states[0]
    upstream = grad_output[0]
    row_count = queries.shape[0]
    features = queries.shape[1]
    inv_root = HD ** (-0.5)
    devices = lax.axis_size("tm")
    bit_count = devices.bit_length() - 1
    top_bit = bit_count - 1
    near_first = {0: 3, 1: 1, 2: 0, 3: 4, 4: 2, 5: 5}
    low_bits = sorted(range(top_bit), key=lambda b: near_first.get(b, b))
    wide = features + 128

    other_qkv = partner(jnp.stack([queries, keys_all, values_all], 0), "tm", 0)
    other_q = other_qkv[0]
    keys_one = jnp.concatenate([keys_all, other_qkv[1]], 0)
    values_one = jnp.concatenate([values_all, other_qkv[2]], 0)
    part_one, lse_one = attend(queries, keys_one, values_one, inv_root)

    qkv = jnp.stack([by_parity(pick_rows(m, R2)) for m in (queries, keys_all, values_all)], 0)
    per_par = qkv.shape[2]
    own = gather_blocks(qkv[:, :, None], 2, low_bits)
    far = partner(own[:, 0], "tm", top_bit)
    q_seg2 = own[0].reshape(-1, features)
    k_seg2 = own[1].reshape(-1, features)
    v_seg2 = own[2].reshape(-1, features)
    q_seg3 = jnp.concatenate([own[0, 0], far[0]], 0).reshape(-1, features)
    k_seg3 = jnp.concatenate([own[1, 0], far[1]], 0).reshape(-1, features)
    v_seg3 = jnp.concatenate([own[2, 0], far[2]], 0).reshape(-1, features)
    q_two = qkv[0].reshape(-1, features)
    q_three = qkv[0, 0]
    part_two, lse_two = attend(q_two, k_seg2, v_seg2, inv_root)
    part_three, lse_three = attend(q_three, k_seg3, v_seg3, inv_root)

    partials = [
        spread_rows(part_one, 1),
        spread_rows(from_parity(part_two.reshape((2, per_par) + part_two.shape[1:])), R2),
        spread_rows(part_three, R3),
    ]
    log_totals = [
        spread_stats(lse_one, 1),
        spread_stats(from_parity(lse_two.reshape(2, per_par, HEADS)), R2),
        spread_stats(lse_three, R3),
    ]
    coverage = [cover_table(row_count, d) for d in (1, R2, R3)]
    merged, weights = merge_levels(log_totals, coverage, partials)
    attn = merged.reshape(row_count, features).astype(jnp.bfloat16)
    output = jnp.dot(attn, out_proj, preferred_element_type=jnp.float32).astype(jnp.bfloat16)
    grad_attn = lax.dot_general(
        upstream, out_proj, (((1,), (1,)), ((), ())), preferred_element_type=jnp.float32
    ).astype(jnp.bfloat16)
    proj_part = lax.dot_general(
        attn, upstream, (((0,), (0,)), ((), ())), preferred_element_type=jnp.float32
    )
    order = (0, 2, 5, 7, 3, 6, 8, 4, 1)
    grad_proj = scatter_sum(proj_part, ("tm", "batch"), order)

    grad_three = grad_attn.astype(jnp.float32).reshape(row_count, HEADS, HD)
    rowdot = jnp.sum(grad_three * merged, axis=2)

    def grad_of(weight_now, grad_rows):
        scaled = weight_now[:, :, None] * grad_rows.astype(jnp.float32).reshape(-1, HEADS, HD)
        return scaled.astype(jnp.bfloat16).reshape(-1, features)

    grad_one = grad_of(weights[0], grad_attn)
    offset_one = weights[0] * rowdot
    packed_one = jnp.concatenate([grad_one, split_exact(jnp.concatenate([lse_one, offset_one], 1))], 1)
    other_one = partner(pad_lanes(packed_one, wide), "tm", 0)
    other_stats = join_exact(other_one[:, features : features + 6 * HEADS])
    total_q = spread_rows(
        near_grad(queries, keys_one, values_one, grad_one, lse_one, offset_one, inv_root), 1
    )
    k_g1, v_g1 = far_grad(
        jnp.concatenate([queries, other_q], 0),
        jnp.concatenate([grad_one, other_one[:, :features]], 0),
        jnp.concatenate([lse_one, other_stats[:, :HEADS]], 0),
        jnp.concatenate([offset_one, other_stats[:, HEADS:]], 0),
        keys_all,
        values_all,
        inv_root,
    )
    total_k = spread_rows(k_g1, 1)
    total_v = spread_rows(v_g1, 1)

    ga_par = by_parity(pick_rows(grad_attn, R2))
    w_two = by_parity(pick_stats(weights[1], R2))
    rd_two = by_parity(pick_stats(rowdot, R2))
    lse_two_par = lse_two.reshape(2, per_par, HEADS)
    w_three = pick_stats(weights[2], R3)
    no_level = jnp.zeros_like(w_three)
    lse3_par = jnp.stack([lse_three, no_level], 0)
    w3_par = jnp.stack([w_three, no_level], 0)
    stats_par = jnp.concatenate([lse_two_par, w_two, lse3_par, w3_par, rd_two], -1)
    packed = pad_lanes(jnp.concatenate([ga_par, split_exact(stats_par)], -1), wide)
    own_b = gather_blocks(packed[:, None], 1, low_bits)
    far_b = partner(own_b[0], "tm", top_bit)
    stat_w = 5 * HEADS

    def unpack(rows):
        rows = rows.reshape(-1, wide)
        stats = join_exact(rows[:, features : features + 3 * stat_w])
        return rows[:, :features], stats.reshape(-1, 5, HEADS)

    g_two = grad_of(w_two.reshape(-1, HEADS), ga_par.reshape(-1, features))
    c_two = w_two.reshape(-1, HEADS) * rd_two.reshape(-1, HEADS)
    grad_q2 = near_grad(q_two, k_seg2, v_seg2, g_two, lse_two, c_two, inv_root)
    ga_seg2, st_seg2 = unpack(own_b)
    k_g2, v_g2 = far_grad(
        q_seg2,
        grad_of(st_seg2[:, 1], ga_seg2),
        st_seg2[:, 0],
        st_seg2[:, 1] * st_seg2[:, 4],
        qkv[1].reshape(-1, features),
        qkv[2].reshape(-1, features),
        inv_root,
    )

    g_three = grad_of(w_three, ga_par[0])
    c_three = w_three * rd_two[0]
    grad_q3 = near_grad(q_three, k_seg3, v_seg3, g_three, lse_three, c_three, inv_root)
    ga_seg3, st_seg3 = unpack(jnp.concatenate([own_b[0], far_b], 0))
    k_g3, v_g3 = far_grad(
        q_seg3,
        grad_of(st_seg3[:, 3], ga_seg3),
        st_seg3[:, 2],
        st_seg3[:, 3] * st_seg3[:, 4],
        qkv[1, 0],
        qkv[2, 0],
        inv_root,
    )

    def level_two_rows(values):
        return spread_rows(from_parity(values.reshape((2, per_par) + values.shape[1:])), R2)

    total_q = total_q + level_two_rows(grad_q2) + spread_rows(grad_q3, R3)
    total_k = total_k + level_two_rows(k_g2) + spread_rows(k_g3, R3)
    total_v = total_v + level_two_rows(v_g2) + spread_rows(v_g3, R3)
    grad_query = total_q.reshape(row_count, features).astype(jnp.bfloat16)
    grad_key = total_k.reshape(row_count, features).astype(jnp.bfloat16)
    grad_value = total_v.reshape(row_count, features).astype(jnp.bfloat16)
    return (output[None], grad_query[None], grad_key[None], grad_value[None], grad_proj)


def solution(mesh):
    in_specs = (
        P("batch", "tm", None),
        P("batch", "tm", None),
        P("batch", "tm", None),
        P(),
        P("batch", "tm", None),
    )
    out_specs = (
        P("batch", "tm", None),
        P("batch", "tm", None),
        P("batch", "tm", None),
        P("batch", "tm", None),
        P(("tm", "batch"), None),
    )
    return jax.shard_map(
        on_device, mesh=mesh, in_specs=in_specs, out_specs=out_specs, check_vma=False
    )
```

```python
import jax
import jax.numpy as jnp
import numpy as np
from jax import lax
from jax.sharding import PartitionSpec as P

HEADS = 8
HD = 64
R2 = 8
R3 = 16


def partner(value, axis, apart):
    mask = 2**apart
    pairs = [(source, source ^ mask) for source in range(lax.axis_size(axis))]
    return lax.ppermute(value, axis, pairs)


def offset_mask(dilation):
    return (np.arange(dilation)[:, None] == (np.arange(HEADS) % dilation)[None, :]).astype(
        np.float32
    )


def cover_table(row_count, dilation):
    return (np.arange(row_count) % dilation)[:, None] == (np.arange(HEADS) % dilation)[None, :]


def pick_rows(matrix, dilation):
    count = matrix.shape[0] // dilation
    blocks = matrix.reshape(count, dilation, HEADS, HD)
    chooser = jnp.asarray(offset_mask(dilation), matrix.dtype)[None, :, :, None]
    return jnp.sum(blocks * chooser, axis=1).reshape(count, HEADS * HD)


def pick_stats(matrix, dilation):
    count = matrix.shape[0] // dilation
    blocks = matrix.reshape(count, dilation, HEADS)
    chooser = jnp.asarray(offset_mask(dilation), matrix.dtype)[None, :, :]
    return jnp.sum(blocks * chooser, axis=1)


def spread_rows(values, dilation):
    chooser = jnp.asarray(offset_mask(dilation), values.dtype)[None, :, :, None]
    return (values[:, None] * chooser).reshape(values.shape[0] * dilation, HEADS, HD)


def spread_stats(values, dilation):
    chooser = jnp.asarray(offset_mask(dilation), values.dtype)[None, :, :]
    return (values[:, None] * chooser).reshape(values.shape[0] * dilation, HEADS)


def merge_levels(log_totals, coverage, partials):
    first_lse = log_totals[0]
    peak = first_lse
    for level_no in range(1, len(log_totals)):
        peak = jnp.maximum(peak, jnp.where(coverage[level_no], log_totals[level_no], first_lse))
    exponents = []
    for level_no in range(len(log_totals)):
        exponents.append(jnp.where(coverage[level_no], jnp.exp(log_totals[level_no] - peak), 0.0))
    denominator = exponents[0]
    for level_no in range(1, len(exponents)):
        denominator = denominator + exponents[level_no]
    weights = []
    merged = None
    for level_no in range(len(exponents)):
        weight_now = exponents[level_no] / denominator
        weights.append(weight_now)
        term = weight_now[:, :, None] * partials[level_no]
        merged = term if merged is None else merged + term
    return (merged, weights)


def gather_blocks(block, axis_pos, bit_order):
    for bit_pos in bit_order:
        block = jnp.concatenate([block, partner(block, "tm", bit_pos)], axis_pos)
    return block


def split_exact(values):
    high = lax.reduce_precision(values, exponent_bits=8, mantissa_bits=7)
    rest = values - high
    middle = lax.reduce_precision(rest, exponent_bits=8, mantissa_bits=7)
    low = rest - middle
    parts = jnp.concatenate([high, middle, low], -1)
    return parts.astype(jnp.bfloat16)


def join_exact(parts):
    width = parts.shape[-1] // 3
    as32 = parts.astype(jnp.float32)
    return as32[..., :width] + (as32[..., width : 2 * width] + as32[..., 2 * width :])


def by_parity(rows):
    return rows.reshape((rows.shape[0] // 2, 2) + rows.shape[1:]).swapaxes(0, 1)


def from_parity(rows):
    return rows.swapaxes(0, 1).reshape((rows.shape[0] * rows.shape[1],) + rows.shape[2:])


def pad_lanes(matrix, width):
    return jnp.pad(matrix, [(0, 0)] * (matrix.ndim - 1) + [(0, width - matrix.shape[-1])])


def scatter_sum(matrix, axes, bit_order):
    index = lax.axis_index(axes)
    bit_count = len(bit_order)
    size = 1 << bit_count
    block = matrix.reshape((2,) * bit_count + matrix.shape[1:])
    dims = [bit_count - 1 - j for j in range(bit_count)]
    for bit_pos in bit_order:
        axis_pos = dims.index(bit_pos)
        my_bit = index // (1 << bit_pos) % 2
        keep = lax.dynamic_index_in_dim(block, my_bit, axis_pos, keepdims=False)
        send = lax.dynamic_index_in_dim(block, 1 - my_bit, axis_pos, keepdims=False)
        pairs = [(source, source ^ (1 << bit_pos)) for source in range(size)]
        block = keep + lax.ppermute(send, axes, pairs)
        dims.pop(axis_pos)
    return block.reshape((1,) + matrix.shape[1:])


def heads_view(matrix):
    return matrix.reshape(matrix.shape[0], HEADS, HD)


def attend(query_rows, key_rows, value_rows, inv_root):
    scores = (
        jnp.einsum(
            "qhd,khd->hqk",
            heads_view(query_rows),
            heads_view(key_rows),
            preferred_element_type=jnp.float32,
        )
        * inv_root
    )
    peak = jnp.max(scores, axis=2, keepdims=True)
    log_total = peak + jnp.log(jnp.sum(jnp.exp(scores - peak), axis=2, keepdims=True))
    weights_bf = jnp.exp(scores - log_total).astype(jnp.bfloat16)
    part_out = jnp.einsum(
        "hqk,khd->qhd", weights_bf, heads_view(value_rows), preferred_element_type=jnp.float32
    )
    return part_out, log_total[:, :, 0].T


def near_grad(query_rows, key_rows, value_rows, grad_rows, lse_rows, offset_rows, inv_root):
    scores = (
        jnp.einsum(
            "qhd,khd->hqk",
            heads_view(query_rows),
            heads_view(key_rows),
            preferred_element_type=jnp.float32,
        )
        * inv_root
    )
    prob_full = jnp.exp(scores - lse_rows.T[:, :, None])
    dprob = jnp.einsum(
        "qhd,khd->hqk",
        heads_view(grad_rows),
        heads_view(value_rows),
        preferred_element_type=jnp.float32,
    )
    dscore = (prob_full * (dprob - offset_rows.T[:, :, None])).astype(jnp.bfloat16)
    return (
        jnp.einsum("hqk,khd->qhd", dscore, heads_view(key_rows), preferred_element_type=jnp.float32)
        * inv_root
    )


def far_grad(query_group, grad_group, lse_group, offset_group, key_rows, value_rows, inv_root):
    scores_far = (
        jnp.einsum(
            "qhd,khd->hqk",
            heads_view(query_group),
            heads_view(key_rows),
            preferred_element_type=jnp.float32,
        )
        * inv_root
    )
    prob_far = jnp.exp(scores_far - lse_group.T[:, :, None])
    grad_v = jnp.einsum(
        "hqk,qhd->khd",
        prob_far.astype(jnp.bfloat16),
        heads_view(grad_group),
        preferred_element_type=jnp.float32,
    )
    dprob_far = jnp.einsum(
        "qhd,khd->hqk",
        heads_view(grad_group),
        heads_view(value_rows),
        preferred_element_type=jnp.float32,
    )
    dscore_far = (prob_far * (dprob_far - offset_group.T[:, :, None])).astype(jnp.bfloat16)
    grad_k = (
        jnp.einsum(
            "hqk,qhd->khd", dscore_far, heads_view(query_group), preferred_element_type=jnp.float32
        )
        * inv_root
    )
    return grad_k, grad_v


def on_device(query_states, key_states, value_states, out_proj, grad_output):
    queries = query_states[0]
    keys_all = key_states[0]
    values_all = value_states[0]
    upstream = grad_output[0]
    row_count = queries.shape[0]
    features = queries.shape[1]
    inv_root = HD ** (-0.5)
    devices = lax.axis_size("tm")
    bit_count = devices.bit_length() - 1
    top_bit = bit_count - 1
    near_first = {0: 3, 1: 1, 2: 0, 3: 4, 4: 2, 5: 5}
    low_bits = sorted(range(top_bit), key=lambda b: near_first.get(b, b))
    wide = features + 128

    other_qkv = partner(jnp.stack([queries, keys_all, values_all], 0), "tm", 0)
    other_q = other_qkv[0]
    keys_one = jnp.concatenate([keys_all, other_qkv[1]], 0)
    values_one = jnp.concatenate([values_all, other_qkv[2]], 0)
    part_one, lse_one = attend(queries, keys_one, values_one, inv_root)

    qkv = jnp.stack([by_parity(pick_rows(m, R2)) for m in (queries, keys_all, values_all)], 0)
    per_par = qkv.shape[2]
    own = gather_blocks(qkv[:, :, None], 2, low_bits)
    far = partner(own[:, 0], "tm", top_bit)
    q_seg2 = own[0].reshape(-1, features)
    k_seg2 = own[1].reshape(-1, features)
    v_seg2 = own[2].reshape(-1, features)
    q_seg3 = jnp.concatenate([own[0, 0], far[0]], 0).reshape(-1, features)
    k_seg3 = jnp.concatenate([own[1, 0], far[1]], 0).reshape(-1, features)
    v_seg3 = jnp.concatenate([own[2, 0], far[2]], 0).reshape(-1, features)
    q_two = qkv[0].reshape(-1, features)
    q_three = qkv[0, 0]
    part_two, lse_two = attend(q_two, k_seg2, v_seg2, inv_root)
    part_three, lse_three = attend(q_three, k_seg3, v_seg3, inv_root)

    partials = [
        spread_rows(part_one, 1),
        spread_rows(from_parity(part_two.reshape((2, per_par) + part_two.shape[1:])), R2),
        spread_rows(part_three, R3),
    ]
    log_totals = [
        spread_stats(lse_one, 1),
        spread_stats(from_parity(lse_two.reshape(2, per_par, HEADS)), R2),
        spread_stats(lse_three, R3),
    ]
    coverage = [cover_table(row_count, d) for d in (1, R2, R3)]
    merged, weights = merge_levels(log_totals, coverage, partials)
    attn = merged.reshape(row_count, features).astype(jnp.bfloat16)
    output = jnp.dot(attn, out_proj, preferred_element_type=jnp.float32).astype(jnp.bfloat16)
    grad_attn = lax.dot_general(
        upstream, out_proj, (((1,), (1,)), ((), ())), preferred_element_type=jnp.float32
    ).astype(jnp.bfloat16)
    proj_part = lax.dot_general(
        attn, upstream, (((0,), (0,)), ((), ())), preferred_element_type=jnp.float32
    )
    order = (0, 2, 5, 7, 3, 6, 8, 4, 1)
    grad_proj = scatter_sum(proj_part, ("tm", "batch"), order)

    grad_three = grad_attn.astype(jnp.float32).reshape(row_count, HEADS, HD)
    rowdot = jnp.sum(grad_three * merged, axis=2)

    def grad_of(weight_now, grad_rows):
        scaled = weight_now[:, :, None] * grad_rows.astype(jnp.float32).reshape(-1, HEADS, HD)
        return scaled.astype(jnp.bfloat16).reshape(-1, features)

    grad_one = grad_of(weights[0], grad_attn)
    offset_one = weights[0] * rowdot
    packed_one = jnp.concatenate([grad_one, split_exact(jnp.concatenate([lse_one, offset_one], 1))], 1)
    other_one = partner(pad_lanes(packed_one, wide), "tm", 0)
    other_stats = join_exact(other_one[:, features : features + 6 * HEADS])
    total_q = spread_rows(
        near_grad(queries, keys_one, values_one, grad_one, lse_one, offset_one, inv_root), 1
    )
    k_g1, v_g1 = far_grad(
        jnp.concatenate([queries, other_q], 0),
        jnp.concatenate([grad_one, other_one[:, :features]], 0),
        jnp.concatenate([lse_one, other_stats[:, :HEADS]], 0),
        jnp.concatenate([offset_one, other_stats[:, HEADS:]], 0),
        keys_all,
        values_all,
        inv_root,
    )
    total_k = spread_rows(k_g1, 1)
    total_v = spread_rows(v_g1, 1)

    ga_par = by_parity(pick_rows(grad_attn, R2))
    w_two = by_parity(pick_stats(weights[1], R2))
    rd_two = by_parity(pick_stats(rowdot, R2))
    lse_two_par = lse_two.reshape(2, per_par, HEADS)
    w_three = pick_stats(weights[2], R3)
    no_level = jnp.zeros_like(w_three)
    lse3_par = jnp.stack([lse_three, no_level], 0)
    w3_par = jnp.stack([w_three, no_level], 0)
    stats_par = jnp.concatenate([lse_two_par, w_two, lse3_par, w3_par, rd_two], -1)
    packed = pad_lanes(jnp.concatenate([ga_par, split_exact(stats_par)], -1), wide)
    own_b = gather_blocks(packed[:, None], 1, low_bits)
    far_b = partner(own_b[0], "tm", top_bit)
    stat_w = 5 * HEADS

    def unpack(rows):
        rows = rows.reshape(-1, wide)
        stats = join_exact(rows[:, features : features + 3 * stat_w])
        return rows[:, :features], stats.reshape(-1, 5, HEADS)

    g_two = grad_of(w_two.reshape(-1, HEADS), ga_par.reshape(-1, features))
    c_two = w_two.reshape(-1, HEADS) * rd_two.reshape(-1, HEADS)
    grad_q2 = near_grad(q_two, k_seg2, v_seg2, g_two, lse_two, c_two, inv_root)
    ga_seg2, st_seg2 = unpack(own_b)
    k_g2, v_g2 = far_grad(
        q_seg2,
        grad_of(st_seg2[:, 1], ga_seg2),
        st_seg2[:, 0],
        st_seg2[:, 1] * st_seg2[:, 4],
        qkv[1].reshape(-1, features),
        qkv[2].reshape(-1, features),
        inv_root,
    )

    g_three = grad_of(w_three, ga_par[0])
    c_three = w_three * rd_two[0]
    grad_q3 = near_grad(q_three, k_seg3, v_seg3, g_three, lse_three, c_three, inv_root)
    ga_seg3, st_seg3 = unpack(jnp.concatenate([own_b[0], far_b], 0))
    k_g3, v_g3 = far_grad(
        q_seg3,
        grad_of(st_seg3[:, 3], ga_seg3),
        st_seg3[:, 2],
        st_seg3[:, 3] * st_seg3[:, 4],
        qkv[1, 0],
        qkv[2, 0],
        inv_root,
    )

    def level_two_rows(values):
        return spread_rows(from_parity(values.reshape((2, per_par) + values.shape[1:])), R2)

    total_q = total_q + level_two_rows(grad_q2) + spread_rows(grad_q3, R3)
    total_k = total_k + level_two_rows(k_g2) + spread_rows(k_g3, R3)
    total_v = total_v + level_two_rows(v_g2) + spread_rows(v_g3, R3)
    grad_query = total_q.reshape(row_count, features).astype(jnp.bfloat16)
    grad_key = total_k.reshape(row_count, features).astype(jnp.bfloat16)
    grad_value = total_v.reshape(row_count, features).astype(jnp.bfloat16)
    return (output[None], grad_query[None], grad_key[None], grad_value[None], grad_proj)


def solution(mesh):
    in_specs = (
        P("batch", "tm", None),
        P("batch", "tm", None),
        P("batch", "tm", None),
        P(),
        P("batch", "tm", None),
    )
    out_specs = (
        P("batch", "tm", None),
        P("batch", "tm", None),
        P("batch", "tm", None),
        P("batch", "tm", None),
        P(("tm", "batch"), None),
    )
    return jax.shard_map(
        on_device, mesh=mesh, in_specs=in_specs, out_specs=out_specs, check_vma=False
    )
```

```python
import jax
import jax.numpy as jnp
import numpy as np
from jax import lax
from jax.sharding import PartitionSpec as P

HEADS = 8
HD = 64
R2 = 8
R3 = 16


def partner(value, axis, apart):
    mask = 2**apart
    pairs = [(source, source ^ mask) for source in range(lax.axis_size(axis))]
    return lax.ppermute(value, axis, pairs)


def offset_mask(dilation):
    return (np.arange(dilation)[:, None] == (np.arange(HEADS) % dilation)[None, :]).astype(
        np.float32
    )


def cover_table(row_count, dilation):
    return (np.arange(row_count) % dilation)[:, None] == (np.arange(HEADS) % dilation)[None, :]


def pick_rows(matrix, dilation):
    count = matrix.shape[0] // dilation
    blocks = matrix.reshape(count, dilation, HEADS, HD)
    chooser = jnp.asarray(offset_mask(dilation), matrix.dtype)[None, :, :, None]
    return jnp.sum(blocks * chooser, axis=1).reshape(count, HEADS * HD)


def pick_stats(matrix, dilation):
    count = matrix.shape[0] // dilation
    blocks = matrix.reshape(count, dilation, HEADS)
    chooser = jnp.asarray(offset_mask(dilation), matrix.dtype)[None, :, :]
    return jnp.sum(blocks * chooser, axis=1)


def spread_rows(values, dilation):
    chooser = jnp.asarray(offset_mask(dilation), values.dtype)[None, :, :, None]
    return (values[:, None] * chooser).reshape(values.shape[0] * dilation, HEADS, HD)


def spread_stats(values, dilation):
    chooser = jnp.asarray(offset_mask(dilation), values.dtype)[None, :, :]
    return (values[:, None] * chooser).reshape(values.shape[0] * dilation, HEADS)


def merge_levels(log_totals, coverage, partials):
    first_lse = log_totals[0]
    peak = first_lse
    for level_no in range(1, len(log_totals)):
        peak = jnp.maximum(peak, jnp.where(coverage[level_no], log_totals[level_no], first_lse))
    exponents = []
    for level_no in range(len(log_totals)):
        exponents.append(jnp.where(coverage[level_no], jnp.exp(log_totals[level_no] - peak), 0.0))
    denominator = exponents[0]
    for level_no in range(1, len(exponents)):
        denominator = denominator + exponents[level_no]
    weights = []
    merged = None
    for level_no in range(len(exponents)):
        weight_now = exponents[level_no] / denominator
        weights.append(weight_now)
        term = weight_now[:, :, None] * partials[level_no]
        merged = term if merged is None else merged + term
    return (merged, weights)


def gather_blocks(block, axis_pos, bit_order):
    for bit_pos in bit_order:
        block = jnp.concatenate([block, partner(block, "tm", bit_pos)], axis_pos)
    return block


def split_exact(values):
    high = lax.reduce_precision(values, exponent_bits=8, mantissa_bits=7)
    rest = values - high
    middle = lax.reduce_precision(rest, exponent_bits=8, mantissa_bits=7)
    low = rest - middle
    parts = jnp.concatenate([high, middle, low], -1)
    return parts.astype(jnp.bfloat16)


def join_exact(parts):
    width = parts.shape[-1] // 3
    as32 = parts.astype(jnp.float32)
    return as32[..., :width] + (as32[..., width : 2 * width] + as32[..., 2 * width :])


def by_parity(rows):
    return rows.reshape((rows.shape[0] // 2, 2) + rows.shape[1:]).swapaxes(0, 1)


def from_parity(rows):
    return rows.swapaxes(0, 1).reshape((rows.shape[0] * rows.shape[1],) + rows.shape[2:])


def pad_lanes(matrix, width):
    return jnp.pad(matrix, [(0, 0)] * (matrix.ndim - 1) + [(0, width - matrix.shape[-1])])


def scatter_sum(matrix, axes, bit_order):
    index = lax.axis_index(axes)
    bit_count = len(bit_order)
    size = 1 << bit_count
    block = matrix.reshape((2,) * bit_count + matrix.shape[1:])
    dims = [bit_count - 1 - j for j in range(bit_count)]
    for bit_pos in bit_order:
        axis_pos = dims.index(bit_pos)
        my_bit = index // (1 << bit_pos) % 2
        keep = lax.dynamic_index_in_dim(block, my_bit, axis_pos, keepdims=False)
        send = lax.dynamic_index_in_dim(block, 1 - my_bit, axis_pos, keepdims=False)
        pairs = [(source, source ^ (1 << bit_pos)) for source in range(size)]
        block = keep + lax.ppermute(send, axes, pairs)
        dims.pop(axis_pos)
    return block.reshape((1,) + matrix.shape[1:])


class HalvingSum:

    def __init__(self, matrix, bit_count):
        self.block = matrix.reshape((2,) * bit_count + matrix.shape[1:])
        self.dims = [bit_count - 1 - j for j in range(bit_count)]
        self.tail = matrix.shape[1:]

    def split(self, bit_pos, my_bit):
        self.axis_pos = self.dims.index(bit_pos)
        self.keep = lax.dynamic_index_in_dim(self.block, my_bit, self.axis_pos, keepdims=False)
        return lax.dynamic_index_in_dim(self.block, 1 - my_bit, self.axis_pos, keepdims=False)

    def absorb(self, received):
        self.block = self.keep + received
        self.dims.pop(self.axis_pos)

    def result(self):
        return self.block.reshape((1,) + self.tail)


def heads_view(matrix):
    return matrix.reshape(matrix.shape[0], HEADS, HD)


def attend(query_rows, key_rows, value_rows, inv_root):
    scores = (
        jnp.einsum(
            "qhd,khd->hqk",
            heads_view(query_rows),
            heads_view(key_rows),
            preferred_element_type=jnp.float32,
        )
        * inv_root
    )
    peak = jnp.max(scores, axis=2, keepdims=True)
    log_total = peak + jnp.log(jnp.sum(jnp.exp(scores - peak), axis=2, keepdims=True))
    weights_bf = jnp.exp(scores - log_total).astype(jnp.bfloat16)
    part_out = jnp.einsum(
        "hqk,khd->qhd", weights_bf, heads_view(value_rows), preferred_element_type=jnp.float32
    )
    return part_out, log_total[:, :, 0].T


def near_grad(query_rows, key_rows, value_rows, grad_rows, lse_rows, offset_rows, inv_root):
    scores = (
        jnp.einsum(
            "qhd,khd->hqk",
            heads_view(query_rows),
            heads_view(key_rows),
            preferred_element_type=jnp.float32,
        )
        * inv_root
    )
    prob_full = jnp.exp(scores - lse_rows.T[:, :, None])
    dprob = jnp.einsum(
        "qhd,khd->hqk",
        heads_view(grad_rows),
        heads_view(value_rows),
        preferred_element_type=jnp.float32,
    )
    dscore = (prob_full * (dprob - offset_rows.T[:, :, None])).astype(jnp.bfloat16)
    return (
        jnp.einsum("hqk,khd->qhd", dscore, heads_view(key_rows), preferred_element_type=jnp.float32)
        * inv_root
    )


def far_grad(query_group, grad_group, lse_group, offset_group, key_rows, value_rows, inv_root):
    scores_far = (
        jnp.einsum(
            "qhd,khd->hqk",
            heads_view(query_group),
            heads_view(key_rows),
            preferred_element_type=jnp.float32,
        )
        * inv_root
    )
    prob_far = jnp.exp(scores_far - lse_group.T[:, :, None])
    grad_v = jnp.einsum(
        "hqk,qhd->khd",
        prob_far.astype(jnp.bfloat16),
        heads_view(grad_group),
        preferred_element_type=jnp.float32,
    )
    dprob_far = jnp.einsum(
        "qhd,khd->hqk",
        heads_view(grad_group),
        heads_view(value_rows),
        preferred_element_type=jnp.float32,
    )
    dscore_far = (prob_far * (dprob_far - offset_group.T[:, :, None])).astype(jnp.bfloat16)
    grad_k = (
        jnp.einsum(
            "hqk,qhd->khd", dscore_far, heads_view(query_group), preferred_element_type=jnp.float32
        )
        * inv_root
    )
    return grad_k, grad_v


def on_device(query_states, key_states, value_states, out_proj, grad_output):
    queries = query_states[0]
    keys_all = key_states[0]
    values_all = value_states[0]
    upstream = grad_output[0]
    row_count = queries.shape[0]
    features = queries.shape[1]
    inv_root = HD ** (-0.5)
    devices = lax.axis_size("tm")
    bit_count = devices.bit_length() - 1
    top_bit = bit_count - 1
    near_first = {0: 3, 1: 1, 2: 0, 3: 4, 4: 2, 5: 5}
    low_bits = sorted(range(top_bit), key=lambda b: near_first.get(b, b))
    wide = features + 128
    wide_b = 2 * features + 128
    back_first = {0: 0, 3: 1, 2: 2, 1: 3, 4: 4, 5: 5}
    back_bits = sorted(range(top_bit), key=lambda b: back_first.get(b, b))
    tm_index = lax.axis_index("tm")
    batch_index = lax.axis_index("batch")
    batch_count = lax.axis_size("batch")
    batch_bits = batch_count.bit_length() - 1

    other_qkv = partner(jnp.stack([queries, keys_all, values_all], 0), "tm", 0)
    other_q = other_qkv[0]
    keys_one = jnp.concatenate([keys_all, other_qkv[1]], 0)
    values_one = jnp.concatenate([values_all, other_qkv[2]], 0)
    part_one, lse_one = attend(queries, keys_one, values_one, inv_root)

    qkv = jnp.stack([by_parity(pick_rows(m, R2)) for m in (queries, keys_all, values_all)], 0)
    per_par = qkv.shape[2]
    own = gather_blocks(qkv[1:, :, None], 2, low_bits)
    far = partner(own[:, 0], "tm", top_bit)
    k_seg2 = own[0].reshape(-1, features)
    v_seg2 = own[1].reshape(-1, features)
    k_seg3 = jnp.concatenate([own[0, 0], far[0]], 0).reshape(-1, features)
    v_seg3 = jnp.concatenate([own[1, 0], far[1]], 0).reshape(-1, features)
    q_two = qkv[0].reshape(-1, features)
    q_three = qkv[0, 0]
    part_two, lse_two = attend(q_two, k_seg2, v_seg2, inv_root)
    part_three, lse_three = attend(q_three, k_seg3, v_seg3, inv_root)

    partials = [
        spread_rows(part_one, 1),
        spread_rows(from_parity(part_two.reshape((2, per_par) + part_two.shape[1:])), R2),
        spread_rows(part_three, R3),
    ]
    log_totals = [
        spread_stats(lse_one, 1),
        spread_stats(from_parity(lse_two.reshape(2, per_par, HEADS)), R2),
        spread_stats(lse_three, R3),
    ]
    coverage = [cover_table(row_count, d) for d in (1, R2, R3)]
    merged, weights = merge_levels(log_totals, coverage, partials)
    attn = merged.reshape(row_count, features).astype(jnp.bfloat16)
    output = jnp.dot(attn, out_proj, preferred_element_type=jnp.float32).astype(jnp.bfloat16)
    grad_attn = lax.dot_general(
        upstream, out_proj, (((1,), (1,)), ((), ())), preferred_element_type=jnp.float32
    ).astype(jnp.bfloat16)
    proj_part = lax.dot_general(
        attn, upstream, (((0,), (0,)), ((), ())), preferred_element_type=jnp.float32
    )
    halving = HalvingSum(proj_part, bit_count + batch_bits)

    def batch_step(bit_pos):
        send = halving.split(bit_pos, batch_index // (1 << bit_pos) % 2)
        pairs = [(s, s ^ (1 << bit_pos)) for s in range(batch_count)]
        halving.absorb(lax.ppermute(send, "batch", pairs))

    def step_with_sum(block, bit_pos):
        send = halving.split(bit_pos + batch_bits, tm_index // (1 << bit_pos) % 2)
        message = jnp.concatenate([block.reshape(-1), split_exact(send.reshape(-1))])
        got = partner(message, "tm", bit_pos)
        halving.absorb(join_exact(got[block.size :]).reshape(send.shape))
        return got[: block.size].reshape(block.shape)

    batch_step(0)

    grad_three = grad_attn.astype(jnp.float32).reshape(row_count, HEADS, HD)
    rowdot = jnp.sum(grad_three * merged, axis=2)

    def grad_of(weight_now, grad_rows):
        scaled = weight_now[:, :, None] * grad_rows.astype(jnp.float32).reshape(-1, HEADS, HD)
        return scaled.astype(jnp.bfloat16).reshape(-1, features)

    grad_one = grad_of(weights[0], grad_attn)
    offset_one = weights[0] * rowdot
    packed_one = jnp.concatenate([grad_one, split_exact(jnp.concatenate([lse_one, offset_one], 1))], 1)
    other_one = partner(pad_lanes(packed_one, wide), "tm", 0)
    other_stats = join_exact(other_one[:, features : features + 6 * HEADS])
    total_q = spread_rows(
        near_grad(queries, keys_one, values_one, grad_one, lse_one, offset_one, inv_root), 1
    )
    k_g1, v_g1 = far_grad(
        jnp.concatenate([queries, other_q], 0),
        jnp.concatenate([grad_one, other_one[:, :features]], 0),
        jnp.concatenate([lse_one, other_stats[:, :HEADS]], 0),
        jnp.concatenate([offset_one, other_stats[:, HEADS:]], 0),
        keys_all,
        values_all,
        inv_root,
    )
    total_k = spread_rows(k_g1, 1)
    total_v = spread_rows(v_g1, 1)

    ga_par = by_parity(pick_rows(grad_attn, R2))
    w_two = by_parity(pick_stats(weights[1], R2))
    rd_two = by_parity(pick_stats(rowdot, R2))
    lse_two_par = lse_two.reshape(2, per_par, HEADS)
    w_three = pick_stats(weights[2], R3)
    no_level = jnp.zeros_like(w_three)
    lse3_par = jnp.stack([lse_three, no_level], 0)
    w3_par = jnp.stack([w_three, no_level], 0)
    stats_par = jnp.concatenate([lse_two_par, w_two, lse3_par, w3_par, rd_two], -1)
    packed = jnp.concatenate([qkv[0], ga_par, split_exact(stats_par)], -1)
    own_b = pad_lanes(packed, wide_b)[:, None]
    for bit_pos in back_bits:
        own_b = jnp.concatenate([own_b, step_with_sum(own_b, bit_pos)], 1)
    far_b = step_with_sum(own_b[0], top_bit)
    for bit_pos in range(1, batch_bits):
        batch_step(bit_pos)
    grad_proj = halving.result()
    stat_w = 5 * HEADS

    def unpack(rows):
        rows = rows.reshape(-1, wide_b)
        stats = join_exact(rows[:, 2 * features : 2 * features + 3 * stat_w])
        return rows[:, :features], rows[:, features : 2 * features], stats.reshape(-1, 5, HEADS)

    g_two = grad_of(w_two.reshape(-1, HEADS), ga_par.reshape(-1, features))
    c_two = w_two.reshape(-1, HEADS) * rd_two.reshape(-1, HEADS)
    grad_q2 = near_grad(q_two, k_seg2, v_seg2, g_two, lse_two, c_two, inv_root)
    q_seg2, ga_seg2, st_seg2 = unpack(own_b)
    k_g2, v_g2 = far_grad(
        q_seg2,
        grad_of(st_seg2[:, 1], ga_seg2),
        st_seg2[:, 0],
        st_seg2[:, 1] * st_seg2[:, 4],
        qkv[1].reshape(-1, features),
        qkv[2].reshape(-1, features),
        inv_root,
    )

    g_three = grad_of(w_three, ga_par[0])
    c_three = w_three * rd_two[0]
    grad_q3 = near_grad(q_three, k_seg3, v_seg3, g_three, lse_three, c_three, inv_root)
    q_seg3, ga_seg3, st_seg3 = unpack(jnp.concatenate([own_b[0], far_b], 0))
    k_g3, v_g3 = far_grad(
        q_seg3,
        grad_of(st_seg3[:, 3], ga_seg3),
        st_seg3[:, 2],
        st_seg3[:, 3] * st_seg3[:, 4],
        qkv[1, 0],
        qkv[2, 0],
        inv_root,
    )

    def level_two_rows(values):
        return spread_rows(from_parity(values.reshape((2, per_par) + values.shape[1:])), R2)

    total_q = total_q + level_two_rows(grad_q2) + spread_rows(grad_q3, R3)
    total_k = total_k + level_two_rows(k_g2) + spread_rows(k_g3, R3)
    total_v = total_v + level_two_rows(v_g2) + spread_rows(v_g3, R3)
    grad_query = total_q.reshape(row_count, features).astype(jnp.bfloat16)
    grad_key = total_k.reshape(row_count, features).astype(jnp.bfloat16)
    grad_value = total_v.reshape(row_count, features).astype(jnp.bfloat16)
    return (output[None], grad_query[None], grad_key[None], grad_value[None], grad_proj)


def solution(mesh):
    in_specs = (
        P("batch", "tm", None),
        P("batch", "tm", None),
        P("batch", "tm", None),
        P(),
        P("batch", "tm", None),
    )
    out_specs = (
        P("batch", "tm", None),
        P("batch", "tm", None),
        P("batch", "tm", None),
        P("batch", "tm", None),
        P(("tm", "batch"), None),
    )
    return jax.shard_map(
        on_device, mesh=mesh, in_specs=in_specs, out_specs=out_specs, check_vma=False
    )
```

```python
import jax
import jax.numpy as jnp
import numpy as np
from jax import lax
from jax.sharding import PartitionSpec as P

HEADS = 8
HD = 64
R2 = 8
R3 = 16


def partner(value, axis, apart):
    mask = 2**apart
    pairs = [(source, source ^ mask) for source in range(lax.axis_size(axis))]
    return lax.ppermute(value, axis, pairs)


def offset_mask(dilation):
    return (np.arange(dilation)[:, None] == (np.arange(HEADS) % dilation)[None, :]).astype(
        np.float32
    )


def cover_table(row_count, dilation):
    return (np.arange(row_count) % dilation)[:, None] == (np.arange(HEADS) % dilation)[None, :]


def pick_rows(matrix, dilation):
    count = matrix.shape[0] // dilation
    blocks = matrix.reshape(count, dilation, HEADS, HD)
    chooser = jnp.asarray(offset_mask(dilation), matrix.dtype)[None, :, :, None]
    return jnp.sum(blocks * chooser, axis=1).reshape(count, HEADS * HD)


def pick_stats(matrix, dilation):
    count = matrix.shape[0] // dilation
    blocks = matrix.reshape(count, dilation, HEADS)
    chooser = jnp.asarray(offset_mask(dilation), matrix.dtype)[None, :, :]
    return jnp.sum(blocks * chooser, axis=1)


def spread_rows(values, dilation):
    chooser = jnp.asarray(offset_mask(dilation), values.dtype)[None, :, :, None]
    return (values[:, None] * chooser).reshape(values.shape[0] * dilation, HEADS, HD)


def spread_stats(values, dilation):
    chooser = jnp.asarray(offset_mask(dilation), values.dtype)[None, :, :]
    return (values[:, None] * chooser).reshape(values.shape[0] * dilation, HEADS)


def merge_levels(log_totals, coverage, partials):
    first_lse = log_totals[0]
    peak = first_lse
    for level_no in range(1, len(log_totals)):
        peak = jnp.maximum(peak, jnp.where(coverage[level_no], log_totals[level_no], first_lse))
    exponents = []
    for level_no in range(len(log_totals)):
        exponents.append(jnp.where(coverage[level_no], jnp.exp(log_totals[level_no] - peak), 0.0))
    denominator = exponents[0]
    for level_no in range(1, len(exponents)):
        denominator = denominator + exponents[level_no]
    weights = []
    merged = None
    for level_no in range(len(exponents)):
        weight_now = exponents[level_no] / denominator
        weights.append(weight_now)
        term = weight_now[:, :, None] * partials[level_no]
        merged = term if merged is None else merged + term
    return (merged, weights)


def gather_blocks(block, axis_pos, bit_order):
    for bit_pos in bit_order:
        block = jnp.concatenate([block, partner(block, "tm", bit_pos)], axis_pos)
    return block


def split_exact(values):
    high = lax.reduce_precision(values, exponent_bits=8, mantissa_bits=7)
    rest = values - high
    middle = lax.reduce_precision(rest, exponent_bits=8, mantissa_bits=7)
    low = rest - middle
    parts = jnp.concatenate([high, middle, low], -1)
    return parts.astype(jnp.bfloat16)


def join_exact(parts):
    width = parts.shape[-1] // 3
    as32 = parts.astype(jnp.float32)
    return as32[..., :width] + (as32[..., width : 2 * width] + as32[..., 2 * width :])


def by_parity(rows):
    return rows.reshape((rows.shape[0] // 2, 2) + rows.shape[1:]).swapaxes(0, 1)


def from_parity(rows):
    return rows.swapaxes(0, 1).reshape((rows.shape[0] * rows.shape[1],) + rows.shape[2:])


def pad_lanes(matrix, width):
    return jnp.pad(matrix, [(0, 0)] * (matrix.ndim - 1) + [(0, width - matrix.shape[-1])])


def scatter_sum(matrix, axes, bit_groups):
    index = lax.axis_index(axes)
    bit_count = sum(len(group) for group in bit_groups)
    size = 1 << bit_count
    block = matrix.reshape((2,) * bit_count + matrix.shape[1:])
    dims = [bit_count - 1 - j for j in range(bit_count)]
    for group in bit_groups:
        low, width = min(group), len(group)
        axis_pos = dims.index(low + width - 1)
        shape = block.shape
        block = block.reshape(shape[:axis_pos] + (1 << width,) + shape[axis_pos + width :])
        mine = index // (1 << low) % (1 << width)
        total = lax.dynamic_index_in_dim(block, mine, axis_pos, keepdims=False)
        for flip in range(1, 1 << width):
            send = lax.dynamic_index_in_dim(block, mine ^ flip, axis_pos, keepdims=False)
            pairs = [(source, source ^ (flip << low)) for source in range(size)]
            total = total + lax.ppermute(send, axes, pairs)
        block = total
        del dims[axis_pos : axis_pos + width]
    return block.reshape((1,) + matrix.shape[1:])


def heads_view(matrix):
    return matrix.reshape(matrix.shape[0], HEADS, HD)


def attend(query_rows, key_rows, value_rows, inv_root):
    scores = (
        jnp.einsum(
            "qhd,khd->hqk",
            heads_view(query_rows),
            heads_view(key_rows),
            preferred_element_type=jnp.float32,
        )
        * inv_root
    )
    peak = jnp.max(scores, axis=2, keepdims=True)
    log_total = peak + jnp.log(jnp.sum(jnp.exp(scores - peak), axis=2, keepdims=True))
    weights_bf = jnp.exp(scores - log_total).astype(jnp.bfloat16)
    part_out = jnp.einsum(
        "hqk,khd->qhd", weights_bf, heads_view(value_rows), preferred_element_type=jnp.float32
    )
    return part_out, log_total[:, :, 0].T


def near_grad(query_rows, key_rows, value_rows, grad_rows, lse_rows, offset_rows, inv_root):
    scores = (
        jnp.einsum(
            "qhd,khd->hqk",
            heads_view(query_rows),
            heads_view(key_rows),
            preferred_element_type=jnp.float32,
        )
        * inv_root
    )
    prob_full = jnp.exp(scores - lse_rows.T[:, :, None])
    dprob = jnp.einsum(
        "qhd,khd->hqk",
        heads_view(grad_rows),
        heads_view(value_rows),
        preferred_element_type=jnp.float32,
    )
    dscore = (prob_full * (dprob - offset_rows.T[:, :, None])).astype(jnp.bfloat16)
    return (
        jnp.einsum("hqk,khd->qhd", dscore, heads_view(key_rows), preferred_element_type=jnp.float32)
        * inv_root
    )


def far_grad(query_group, grad_group, lse_group, offset_group, key_rows, value_rows, inv_root):
    scores_far = (
        jnp.einsum(
            "qhd,khd->hqk",
            heads_view(query_group),
            heads_view(key_rows),
            preferred_element_type=jnp.float32,
        )
        * inv_root
    )
    prob_far = jnp.exp(scores_far - lse_group.T[:, :, None])
    grad_v = jnp.einsum(
        "hqk,qhd->khd",
        prob_far.astype(jnp.bfloat16),
        heads_view(grad_group),
        preferred_element_type=jnp.float32,
    )
    dprob_far = jnp.einsum(
        "qhd,khd->hqk",
        heads_view(grad_group),
        heads_view(value_rows),
        preferred_element_type=jnp.float32,
    )
    dscore_far = (prob_far * (dprob_far - offset_group.T[:, :, None])).astype(jnp.bfloat16)
    grad_k = (
        jnp.einsum(
            "hqk,qhd->khd", dscore_far, heads_view(query_group), preferred_element_type=jnp.float32
        )
        * inv_root
    )
    return grad_k, grad_v


def on_device(query_states, key_states, value_states, out_proj, grad_output):
    queries = query_states[0]
    keys_all = key_states[0]
    values_all = value_states[0]
    upstream = grad_output[0]
    row_count = queries.shape[0]
    features = queries.shape[1]
    inv_root = HD ** (-0.5)
    devices = lax.axis_size("tm")
    bit_count = devices.bit_length() - 1
    top_bit = bit_count - 1
    near_first = {0: 3, 1: 1, 2: 0, 3: 4, 4: 2, 5: 5}
    low_bits = sorted(range(top_bit), key=lambda b: near_first.get(b, b))
    wide = features + 128

    other_qkv = partner(jnp.stack([queries, keys_all, values_all], 0), "tm", 0)
    other_q = other_qkv[0]
    keys_one = jnp.concatenate([keys_all, other_qkv[1]], 0)
    values_one = jnp.concatenate([values_all, other_qkv[2]], 0)
    part_one, lse_one = attend(queries, keys_one, values_one, inv_root)

    qkv = jnp.stack([by_parity(pick_rows(m, R2)) for m in (queries, keys_all, values_all)], 0)
    per_par = qkv.shape[2]
    own = gather_blocks(qkv[:, :, None], 2, low_bits)
    far = partner(own[:, 0], "tm", top_bit)
    q_seg2 = own[0].reshape(-1, features)
    k_seg2 = own[1].reshape(-1, features)
    v_seg2 = own[2].reshape(-1, features)
    q_seg3 = jnp.concatenate([own[0, 0], far[0]], 0).reshape(-1, features)
    k_seg3 = jnp.concatenate([own[1, 0], far[1]], 0).reshape(-1, features)
    v_seg3 = jnp.concatenate([own[2, 0], far[2]], 0).reshape(-1, features)
    q_two = qkv[0].reshape(-1, features)
    q_three = qkv[0, 0]
    part_two, lse_two = attend(q_two, k_seg2, v_seg2, inv_root)
    part_three, lse_three = attend(q_three, k_seg3, v_seg3, inv_root)

    partials = [
        spread_rows(part_one, 1),
        spread_rows(from_parity(part_two.reshape((2, per_par) + part_two.shape[1:])), R2),
        spread_rows(part_three, R3),
    ]
    log_totals = [
        spread_stats(lse_one, 1),
        spread_stats(from_parity(lse_two.reshape(2, per_par, HEADS)), R2),
        spread_stats(lse_three, R3),
    ]
    coverage = [cover_table(row_count, d) for d in (1, R2, R3)]
    merged, weights = merge_levels(log_totals, coverage, partials)
    attn = merged.reshape(row_count, features).astype(jnp.bfloat16)
    output = jnp.dot(attn, out_proj, preferred_element_type=jnp.float32).astype(jnp.bfloat16)
    grad_attn = lax.dot_general(
        upstream, out_proj, (((1,), (1,)), ((), ())), preferred_element_type=jnp.float32
    ).astype(jnp.bfloat16)
    proj_part = lax.dot_general(
        attn, upstream, (((0,), (0,)), ((), ())), preferred_element_type=jnp.float32
    )
    order = ((0,), (2,), (5, 6), (7, 8), (3,), (4,), (1,))
    grad_proj = scatter_sum(proj_part, ("tm", "batch"), order)

    grad_three = grad_attn.astype(jnp.float32).reshape(row_count, HEADS, HD)
    rowdot = jnp.sum(grad_three * merged, axis=2)

    def grad_of(weight_now, grad_rows):
        scaled = weight_now[:, :, None] * grad_rows.astype(jnp.float32).reshape(-1, HEADS, HD)
        return scaled.astype(jnp.bfloat16).reshape(-1, features)

    grad_one = grad_of(weights[0], grad_attn)
    offset_one = weights[0] * rowdot
    packed_one = jnp.concatenate([grad_one, split_exact(jnp.concatenate([lse_one, offset_one], 1))], 1)
    other_one = partner(pad_lanes(packed_one, wide), "tm", 0)
    other_stats = join_exact(other_one[:, features : features + 6 * HEADS])
    total_q = spread_rows(
        near_grad(queries, keys_one, values_one, grad_one, lse_one, offset_one, inv_root), 1
    )
    k_g1, v_g1 = far_grad(
        jnp.concatenate([queries, other_q], 0),
        jnp.concatenate([grad_one, other_one[:, :features]], 0),
        jnp.concatenate([lse_one, other_stats[:, :HEADS]], 0),
        jnp.concatenate([offset_one, other_stats[:, HEADS:]], 0),
        keys_all,
        values_all,
        inv_root,
    )
    total_k = spread_rows(k_g1, 1)
    total_v = spread_rows(v_g1, 1)

    ga_par = by_parity(pick_rows(grad_attn, R2))
    w_two = by_parity(pick_stats(weights[1], R2))
    rd_two = by_parity(pick_stats(rowdot, R2))
    lse_two_par = lse_two.reshape(2, per_par, HEADS)
    w_three = pick_stats(weights[2], R3)
    no_level = jnp.zeros_like(w_three)
    lse3_par = jnp.stack([lse_three, no_level], 0)
    w3_par = jnp.stack([w_three, no_level], 0)
    stats_par = jnp.concatenate([lse_two_par, w_two, lse3_par, w3_par, rd_two], -1)
    packed = pad_lanes(jnp.concatenate([ga_par, split_exact(stats_par)], -1), wide)
    own_b = gather_blocks(packed[:, None], 1, low_bits)
    far_b = partner(own_b[0], "tm", top_bit)
    stat_w = 5 * HEADS

    def unpack(rows):
        rows = rows.reshape(-1, wide)
        stats = join_exact(rows[:, features : features + 3 * stat_w])
        return rows[:, :features], stats.reshape(-1, 5, HEADS)

    g_two = grad_of(w_two.reshape(-1, HEADS), ga_par.reshape(-1, features))
    c_two = w_two.reshape(-1, HEADS) * rd_two.reshape(-1, HEADS)
    grad_q2 = near_grad(q_two, k_seg2, v_seg2, g_two, lse_two, c_two, inv_root)
    ga_seg2, st_seg2 = unpack(own_b)
    k_g2, v_g2 = far_grad(
        q_seg2,
        grad_of(st_seg2[:, 1], ga_seg2),
        st_seg2[:, 0],
        st_seg2[:, 1] * st_seg2[:, 4],
        qkv[1].reshape(-1, features),
        qkv[2].reshape(-1, features),
        inv_root,
    )

    g_three = grad_of(w_three, ga_par[0])
    c_three = w_three * rd_two[0]
    grad_q3 = near_grad(q_three, k_seg3, v_seg3, g_three, lse_three, c_three, inv_root)
    ga_seg3, st_seg3 = unpack(jnp.concatenate([own_b[0], far_b], 0))
    k_g3, v_g3 = far_grad(
        q_seg3,
        grad_of(st_seg3[:, 3], ga_seg3),
        st_seg3[:, 2],
        st_seg3[:, 3] * st_seg3[:, 4],
        qkv[1, 0],
        qkv[2, 0],
        inv_root,
    )

    def level_two_rows(values):
        return spread_rows(from_parity(values.reshape((2, per_par) + values.shape[1:])), R2)

    total_q = total_q + level_two_rows(grad_q2) + spread_rows(grad_q3, R3)
    total_k = total_k + level_two_rows(k_g2) + spread_rows(k_g3, R3)
    total_v = total_v + level_two_rows(v_g2) + spread_rows(v_g3, R3)
    grad_query = total_q.reshape(row_count, features).astype(jnp.bfloat16)
    grad_key = total_k.reshape(row_count, features).astype(jnp.bfloat16)
    grad_value = total_v.reshape(row_count, features).astype(jnp.bfloat16)
    return (output[None], grad_query[None], grad_key[None], grad_value[None], grad_proj)


def solution(mesh):
    in_specs = (
        P("batch", "tm", None),
        P("batch", "tm", None),
        P("batch", "tm", None),
        P(),
        P("batch", "tm", None),
    )
    out_specs = (
        P("batch", "tm", None),
        P("batch", "tm", None),
        P("batch", "tm", None),
        P("batch", "tm", None),
        P(("tm", "batch"), None),
    )
    return jax.shard_map(
        on_device, mesh=mesh, in_specs=in_specs, out_specs=out_specs, check_vma=False
    )
```

```python
import jax
import jax.numpy as jnp
import numpy as np
from jax import lax
from jax.sharding import PartitionSpec as P

HEADS = 8
HD = 64
R2 = 8
R3 = 16


def partner(value, axis, apart):
    mask = 2**apart
    pairs = [(source, source ^ mask) for source in range(lax.axis_size(axis))]
    return lax.ppermute(value, axis, pairs)


def offset_mask(dilation):
    return (np.arange(dilation)[:, None] == (np.arange(HEADS) % dilation)[None, :]).astype(
        np.float32
    )


def cover_table(row_count, dilation):
    return (np.arange(row_count) % dilation)[:, None] == (np.arange(HEADS) % dilation)[None, :]


def pick_rows(matrix, dilation):
    count = matrix.shape[0] // dilation
    blocks = matrix.reshape(count, dilation, HEADS, HD)
    chooser = jnp.asarray(offset_mask(dilation), matrix.dtype)[None, :, :, None]
    return jnp.sum(blocks * chooser, axis=1).reshape(count, HEADS * HD)


def pick_stats(matrix, dilation):
    count = matrix.shape[0] // dilation
    blocks = matrix.reshape(count, dilation, HEADS)
    chooser = jnp.asarray(offset_mask(dilation), matrix.dtype)[None, :, :]
    return jnp.sum(blocks * chooser, axis=1)


def spread_rows(values, dilation):
    chooser = jnp.asarray(offset_mask(dilation), values.dtype)[None, :, :, None]
    return (values[:, None] * chooser).reshape(values.shape[0] * dilation, HEADS, HD)


def spread_stats(values, dilation):
    chooser = jnp.asarray(offset_mask(dilation), values.dtype)[None, :, :]
    return (values[:, None] * chooser).reshape(values.shape[0] * dilation, HEADS)


def merge_levels(log_totals, coverage, partials):
    first_lse = log_totals[0]
    peak = first_lse
    for level_no in range(1, len(log_totals)):
        peak = jnp.maximum(peak, jnp.where(coverage[level_no], log_totals[level_no], first_lse))
    exponents = []
    for level_no in range(len(log_totals)):
        exponents.append(jnp.where(coverage[level_no], jnp.exp(log_totals[level_no] - peak), 0.0))
    denominator = exponents[0]
    for level_no in range(1, len(exponents)):
        denominator = denominator + exponents[level_no]
    weights = []
    merged = None
    for level_no in range(len(exponents)):
        weight_now = exponents[level_no] / denominator
        weights.append(weight_now)
        term = weight_now[:, :, None] * partials[level_no]
        merged = term if merged is None else merged + term
    return (merged, weights)


def gather_blocks(block, axis_pos, bit_groups):
    devices = lax.axis_size("tm")
    for group in bit_groups:
        pieces = [block]
        for flip in range(1, 1 << len(group)):
            mask = sum(((flip >> t) & 1) << bit_pos for t, bit_pos in enumerate(group))
            pairs = [(source, source ^ mask) for source in range(devices)]
            pieces.append(lax.ppermute(block, "tm", pairs))
        block = jnp.concatenate(pieces, axis_pos)
    return block


def split_exact(values):
    high = lax.reduce_precision(values, exponent_bits=8, mantissa_bits=7)
    rest = values - high
    middle = lax.reduce_precision(rest, exponent_bits=8, mantissa_bits=7)
    low = rest - middle
    parts = jnp.concatenate([high, middle, low], -1)
    return parts.astype(jnp.bfloat16)


def join_exact(parts):
    width = parts.shape[-1] // 3
    as32 = parts.astype(jnp.float32)
    return as32[..., :width] + (as32[..., width : 2 * width] + as32[..., 2 * width :])


def by_parity(rows):
    return rows.reshape((rows.shape[0] // 2, 2) + rows.shape[1:]).swapaxes(0, 1)


def from_parity(rows):
    return rows.swapaxes(0, 1).reshape((rows.shape[0] * rows.shape[1],) + rows.shape[2:])


def pad_lanes(matrix, width):
    return jnp.pad(matrix, [(0, 0)] * (matrix.ndim - 1) + [(0, width - matrix.shape[-1])])


def scatter_sum(matrix, axes, bit_order):
    index = lax.axis_index(axes)
    bit_count = len(bit_order)
    size = 1 << bit_count
    block = matrix.reshape((2,) * bit_count + matrix.shape[1:])
    dims = [bit_count - 1 - j for j in range(bit_count)]
    for bit_pos in bit_order:
        axis_pos = dims.index(bit_pos)
        my_bit = index // (1 << bit_pos) % 2
        keep = lax.dynamic_index_in_dim(block, my_bit, axis_pos, keepdims=False)
        send = lax.dynamic_index_in_dim(block, 1 - my_bit, axis_pos, keepdims=False)
        pairs = [(source, source ^ (1 << bit_pos)) for source in range(size)]
        block = keep + lax.ppermute(send, axes, pairs)
        dims.pop(axis_pos)
    return block.reshape((1,) + matrix.shape[1:])


def heads_view(matrix):
    return matrix.reshape(matrix.shape[0], HEADS, HD)


def attend(query_rows, key_rows, value_rows, inv_root):
    scores = (
        jnp.einsum(
            "qhd,khd->hqk",
            heads_view(query_rows),
            heads_view(key_rows),
            preferred_element_type=jnp.float32,
        )
        * inv_root
    )
    peak = jnp.max(scores, axis=2, keepdims=True)
    log_total = peak + jnp.log(jnp.sum(jnp.exp(scores - peak), axis=2, keepdims=True))
    weights_bf = jnp.exp(scores - log_total).astype(jnp.bfloat16)
    part_out = jnp.einsum(
        "hqk,khd->qhd", weights_bf, heads_view(value_rows), preferred_element_type=jnp.float32
    )
    return part_out, log_total[:, :, 0].T


def near_grad(query_rows, key_rows, value_rows, grad_rows, lse_rows, offset_rows, inv_root):
    scores = (
        jnp.einsum(
            "qhd,khd->hqk",
            heads_view(query_rows),
            heads_view(key_rows),
            preferred_element_type=jnp.float32,
        )
        * inv_root
    )
    prob_full = jnp.exp(scores - lse_rows.T[:, :, None])
    dprob = jnp.einsum(
        "qhd,khd->hqk",
        heads_view(grad_rows),
        heads_view(value_rows),
        preferred_element_type=jnp.float32,
    )
    dscore = (prob_full * (dprob - offset_rows.T[:, :, None])).astype(jnp.bfloat16)
    return (
        jnp.einsum("hqk,khd->qhd", dscore, heads_view(key_rows), preferred_element_type=jnp.float32)
        * inv_root
    )


def far_grad(query_group, grad_group, lse_group, offset_group, key_rows, value_rows, inv_root):
    scores_far = (
        jnp.einsum(
            "qhd,khd->hqk",
            heads_view(query_group),
            heads_view(key_rows),
            preferred_element_type=jnp.float32,
        )
        * inv_root
    )
    prob_far = jnp.exp(scores_far - lse_group.T[:, :, None])
    grad_v = jnp.einsum(
        "hqk,qhd->khd",
        prob_far.astype(jnp.bfloat16),
        heads_view(grad_group),
        preferred_element_type=jnp.float32,
    )
    dprob_far = jnp.einsum(
        "qhd,khd->hqk",
        heads_view(grad_group),
        heads_view(value_rows),
        preferred_element_type=jnp.float32,
    )
    dscore_far = (prob_far * (dprob_far - offset_group.T[:, :, None])).astype(jnp.bfloat16)
    grad_k = (
        jnp.einsum(
            "hqk,qhd->khd", dscore_far, heads_view(query_group), preferred_element_type=jnp.float32
        )
        * inv_root
    )
    return grad_k, grad_v


def on_device(query_states, key_states, value_states, out_proj, grad_output):
    queries = query_states[0]
    keys_all = key_states[0]
    values_all = value_states[0]
    upstream = grad_output[0]
    row_count = queries.shape[0]
    features = queries.shape[1]
    inv_root = HD ** (-0.5)
    devices = lax.axis_size("tm")
    bit_count = devices.bit_length() - 1
    top_bit = bit_count - 1
    low_bits = ((2,), (1,), (0,), (3, 4), (5,))
    wide = features + 128

    other_qkv = partner(jnp.stack([queries, keys_all, values_all], 0), "tm", 0)
    other_q = other_qkv[0]
    keys_one = jnp.concatenate([keys_all, other_qkv[1]], 0)
    values_one = jnp.concatenate([values_all, other_qkv[2]], 0)
    part_one, lse_one = attend(queries, keys_one, values_one, inv_root)

    qkv = jnp.stack([by_parity(pick_rows(m, R2)) for m in (queries, keys_all, values_all)], 0)
    per_par = qkv.shape[2]
    own = gather_blocks(qkv[:, :, None], 2, low_bits)
    far = partner(own[:, 0], "tm", top_bit)
    q_seg2 = own[0].reshape(-1, features)
    k_seg2 = own[1].reshape(-1, features)
    v_seg2 = own[2].reshape(-1, features)
    q_seg3 = jnp.concatenate([own[0, 0], far[0]], 0).reshape(-1, features)
    k_seg3 = jnp.concatenate([own[1, 0], far[1]], 0).reshape(-1, features)
    v_seg3 = jnp.concatenate([own[2, 0], far[2]], 0).reshape(-1, features)
    q_two = qkv[0].reshape(-1, features)
    q_three = qkv[0, 0]
    part_two, lse_two = attend(q_two, k_seg2, v_seg2, inv_root)
    part_three, lse_three = attend(q_three, k_seg3, v_seg3, inv_root)

    partials = [
        spread_rows(part_one, 1),
        spread_rows(from_parity(part_two.reshape((2, per_par) + part_two.shape[1:])), R2),
        spread_rows(part_three, R3),
    ]
    log_totals = [
        spread_stats(lse_one, 1),
        spread_stats(from_parity(lse_two.reshape(2, per_par, HEADS)), R2),
        spread_stats(lse_three, R3),
    ]
    coverage = [cover_table(row_count, d) for d in (1, R2, R3)]
    merged, weights = merge_levels(log_totals, coverage, partials)
    attn = merged.reshape(row_count, features).astype(jnp.bfloat16)
    output = jnp.dot(attn, out_proj, preferred_element_type=jnp.float32).astype(jnp.bfloat16)
    grad_attn = lax.dot_general(
        upstream, out_proj, (((1,), (1,)), ((), ())), preferred_element_type=jnp.float32
    ).astype(jnp.bfloat16)
    proj_part = lax.dot_general(
        attn, upstream, (((0,), (0,)), ((), ())), preferred_element_type=jnp.float32
    )
    order = (0, 2, 5, 7, 3, 6, 8, 4, 1)
    grad_proj = scatter_sum(proj_part, ("tm", "batch"), order)

    grad_three = grad_attn.astype(jnp.float32).reshape(row_count, HEADS, HD)
    rowdot = jnp.sum(grad_three * merged, axis=2)

    def grad_of(weight_now, grad_rows):
        scaled = weight_now[:, :, None] * grad_rows.astype(jnp.float32).reshape(-1, HEADS, HD)
        return scaled.astype(jnp.bfloat16).reshape(-1, features)

    grad_one = grad_of(weights[0], grad_attn)
    offset_one = weights[0] * rowdot
    packed_one = jnp.concatenate([grad_one, split_exact(jnp.concatenate([lse_one, offset_one], 1))], 1)
    other_one = partner(pad_lanes(packed_one, wide), "tm", 0)
    other_stats = join_exact(other_one[:, features : features + 6 * HEADS])
    total_q = spread_rows(
        near_grad(queries, keys_one, values_one, grad_one, lse_one, offset_one, inv_root), 1
    )
    k_g1, v_g1 = far_grad(
        jnp.concatenate([queries, other_q], 0),
        jnp.concatenate([grad_one, other_one[:, :features]], 0),
        jnp.concatenate([lse_one, other_stats[:, :HEADS]], 0),
        jnp.concatenate([offset_one, other_stats[:, HEADS:]], 0),
        keys_all,
        values_all,
        inv_root,
    )
    total_k = spread_rows(k_g1, 1)
    total_v = spread_rows(v_g1, 1)

    ga_par = by_parity(pick_rows(grad_attn, R2))
    w_two = by_parity(pick_stats(weights[1], R2))
    rd_two = by_parity(pick_stats(rowdot, R2))
    lse_two_par = lse_two.reshape(2, per_par, HEADS)
    w_three = pick_stats(weights[2], R3)
    no_level = jnp.zeros_like(w_three)
    lse3_par = jnp.stack([lse_three, no_level], 0)
    w3_par = jnp.stack([w_three, no_level], 0)
    stats_par = jnp.concatenate([lse_two_par, w_two, lse3_par, w3_par, rd_two], -1)
    packed = pad_lanes(jnp.concatenate([ga_par, split_exact(stats_par)], -1), wide)
    own_b = gather_blocks(packed[:, None], 1, low_bits)
    far_b = partner(own_b[0], "tm", top_bit)
    stat_w = 5 * HEADS

    def unpack(rows):
        rows = rows.reshape(-1, wide)
        stats = join_exact(rows[:, features : features + 3 * stat_w])
        return rows[:, :features], stats.reshape(-1, 5, HEADS)

    g_two = grad_of(w_two.reshape(-1, HEADS), ga_par.reshape(-1, features))
    c_two = w_two.reshape(-1, HEADS) * rd_two.reshape(-1, HEADS)
    grad_q2 = near_grad(q_two, k_seg2, v_seg2, g_two, lse_two, c_two, inv_root)
    ga_seg2, st_seg2 = unpack(own_b)
    k_g2, v_g2 = far_grad(
        q_seg2,
        grad_of(st_seg2[:, 1], ga_seg2),
        st_seg2[:, 0],
        st_seg2[:, 1] * st_seg2[:, 4],
        qkv[1].reshape(-1, features),
        qkv[2].reshape(-1, features),
        inv_root,
    )

    g_three = grad_of(w_three, ga_par[0])
    c_three = w_three * rd_two[0]
    grad_q3 = near_grad(q_three, k_seg3, v_seg3, g_three, lse_three, c_three, inv_root)
    ga_seg3, st_seg3 = unpack(jnp.concatenate([own_b[0], far_b], 0))
    k_g3, v_g3 = far_grad(
        q_seg3,
        grad_of(st_seg3[:, 3], ga_seg3),
        st_seg3[:, 2],
        st_seg3[:, 3] * st_seg3[:, 4],
        qkv[1, 0],
        qkv[2, 0],
        inv_root,
    )

    def level_two_rows(values):
        return spread_rows(from_parity(values.reshape((2, per_par) + values.shape[1:])), R2)

    total_q = total_q + level_two_rows(grad_q2) + spread_rows(grad_q3, R3)
    total_k = total_k + level_two_rows(k_g2) + spread_rows(k_g3, R3)
    total_v = total_v + level_two_rows(v_g2) + spread_rows(v_g3, R3)
    grad_query = total_q.reshape(row_count, features).astype(jnp.bfloat16)
    grad_key = total_k.reshape(row_count, features).astype(jnp.bfloat16)
    grad_value = total_v.reshape(row_count, features).astype(jnp.bfloat16)
    return (output[None], grad_query[None], grad_key[None], grad_value[None], grad_proj)


def solution(mesh):
    in_specs = (
        P("batch", "tm", None),
        P("batch", "tm", None),
        P("batch", "tm", None),
        P(),
        P("batch", "tm", None),
    )
    out_specs = (
        P("batch", "tm", None),
        P("batch", "tm", None),
        P("batch", "tm", None),
        P("batch", "tm", None),
        P(("tm", "batch"), None),
    )
    return jax.shard_map(
        on_device, mesh=mesh, in_specs=in_specs, out_specs=out_specs, check_vma=False
    )
```

```python
import jax
import jax.numpy as jnp
import numpy as np
from jax import lax
from jax.sharding import PartitionSpec as P

HEADS = 8
HD = 64
R2 = 8
R3 = 16


def partner(value, axis, apart):
    mask = 2**apart
    pairs = [(source, source ^ mask) for source in range(lax.axis_size(axis))]
    return lax.ppermute(value, axis, pairs)


def offset_mask(dilation):
    return (np.arange(dilation)[:, None] == (np.arange(HEADS) % dilation)[None, :]).astype(
        np.float32
    )


def cover_table(row_count, dilation):
    return (np.arange(row_count) % dilation)[:, None] == (np.arange(HEADS) % dilation)[None, :]


def pick_rows(matrix, dilation):
    count = matrix.shape[0] // dilation
    blocks = matrix.reshape(count, dilation, HEADS, HD)
    chooser = jnp.asarray(offset_mask(dilation), matrix.dtype)[None, :, :, None]
    return jnp.sum(blocks * chooser, axis=1).reshape(count, HEADS * HD)


def pick_stats(matrix, dilation):
    count = matrix.shape[0] // dilation
    blocks = matrix.reshape(count, dilation, HEADS)
    chooser = jnp.asarray(offset_mask(dilation), matrix.dtype)[None, :, :]
    return jnp.sum(blocks * chooser, axis=1)


def spread_rows(values, dilation):
    chooser = jnp.asarray(offset_mask(dilation), values.dtype)[None, :, :, None]
    return (values[:, None] * chooser).reshape(values.shape[0] * dilation, HEADS, HD)


def spread_stats(values, dilation):
    chooser = jnp.asarray(offset_mask(dilation), values.dtype)[None, :, :]
    return (values[:, None] * chooser).reshape(values.shape[0] * dilation, HEADS)


def merge_levels(log_totals, coverage, partials):
    first_lse = log_totals[0]
    peak = first_lse
    for level_no in range(1, len(log_totals)):
        peak = jnp.maximum(peak, jnp.where(coverage[level_no], log_totals[level_no], first_lse))
    exponents = []
    for level_no in range(len(log_totals)):
        exponents.append(jnp.where(coverage[level_no], jnp.exp(log_totals[level_no] - peak), 0.0))
    denominator = exponents[0]
    for level_no in range(1, len(exponents)):
        denominator = denominator + exponents[level_no]
    weights = []
    merged = None
    for level_no in range(len(exponents)):
        weight_now = exponents[level_no] / denominator
        weights.append(weight_now)
        term = weight_now[:, :, None] * partials[level_no]
        merged = term if merged is None else merged + term
    return (merged, weights)


def gather_blocks(block, axis_pos, bit_order):
    for bit_pos in bit_order:
        block = jnp.concatenate([block, partner(block, "tm", bit_pos)], axis_pos)
    return block


def gather_with_rider(block, axis_pos, bit_order, rider):
    lanes = block.shape[-1]
    for bit_pos in bit_order:
        if bit_pos == 0:
            rows = block.size // lanes
            message = jnp.concatenate([block.reshape(rows, lanes), rider.reshape(-1, lanes)], 0)
            got = partner(message, "tm", bit_pos)
            other = got[:rows].reshape(block.shape)
            rider_back = got[rows:].reshape(rider.shape)
        else:
            other = partner(block, "tm", bit_pos)
        block = jnp.concatenate([block, other], axis_pos)
    return block, rider_back


def split_exact(values):
    high = lax.reduce_precision(values, exponent_bits=8, mantissa_bits=7)
    rest = values - high
    middle = lax.reduce_precision(rest, exponent_bits=8, mantissa_bits=7)
    low = rest - middle
    parts = jnp.concatenate([high, middle, low], -1)
    return parts.astype(jnp.bfloat16)


def join_exact(parts):
    width = parts.shape[-1] // 3
    as32 = parts.astype(jnp.float32)
    return as32[..., :width] + (as32[..., width : 2 * width] + as32[..., 2 * width :])


def by_parity(rows):
    return rows.reshape((rows.shape[0] // 2, 2) + rows.shape[1:]).swapaxes(0, 1)


def from_parity(rows):
    return rows.swapaxes(0, 1).reshape((rows.shape[0] * rows.shape[1],) + rows.shape[2:])


def pad_lanes(matrix, width):
    return jnp.pad(matrix, [(0, 0)] * (matrix.ndim - 1) + [(0, width - matrix.shape[-1])])


def scatter_sum(matrix, axes, bit_order):
    index = lax.axis_index(axes)
    bit_count = len(bit_order)
    size = 1 << bit_count
    block = matrix.reshape((2,) * bit_count + matrix.shape[1:])
    dims = [bit_count - 1 - j for j in range(bit_count)]
    for bit_pos in bit_order:
        axis_pos = dims.index(bit_pos)
        my_bit = index // (1 << bit_pos) % 2
        keep = lax.dynamic_index_in_dim(block, my_bit, axis_pos, keepdims=False)
        send = lax.dynamic_index_in_dim(block, 1 - my_bit, axis_pos, keepdims=False)
        pairs = [(source, source ^ (1 << bit_pos)) for source in range(size)]
        block = keep + lax.ppermute(send, axes, pairs)
        dims.pop(axis_pos)
    return block.reshape((1,) + matrix.shape[1:])


def heads_view(matrix):
    return matrix.reshape(matrix.shape[0], HEADS, HD)


def attend(query_rows, key_rows, value_rows, inv_root):
    scores = (
        jnp.einsum(
            "qhd,khd->hqk",
            heads_view(query_rows),
            heads_view(key_rows),
            preferred_element_type=jnp.float32,
        )
        * inv_root
    )
    peak = jnp.max(scores, axis=2, keepdims=True)
    log_total = peak + jnp.log(jnp.sum(jnp.exp(scores - peak), axis=2, keepdims=True))
    weights_bf = jnp.exp(scores - log_total).astype(jnp.bfloat16)
    part_out = jnp.einsum(
        "hqk,khd->qhd", weights_bf, heads_view(value_rows), preferred_element_type=jnp.float32
    )
    return part_out, log_total[:, :, 0].T


def near_grad(query_rows, key_rows, value_rows, grad_rows, lse_rows, offset_rows, inv_root):
    scores = (
        jnp.einsum(
            "qhd,khd->hqk",
            heads_view(query_rows),
            heads_view(key_rows),
            preferred_element_type=jnp.float32,
        )
        * inv_root
    )
    prob_full = jnp.exp(scores - lse_rows.T[:, :, None])
    dprob = jnp.einsum(
        "qhd,khd->hqk",
        heads_view(grad_rows),
        heads_view(value_rows),
        preferred_element_type=jnp.float32,
    )
    dscore = (prob_full * (dprob - offset_rows.T[:, :, None])).astype(jnp.bfloat16)
    return (
        jnp.einsum("hqk,khd->qhd", dscore, heads_view(key_rows), preferred_element_type=jnp.float32)
        * inv_root
    )


def far_grad(query_group, grad_group, lse_group, offset_group, key_rows, value_rows, inv_root):
    scores_far = (
        jnp.einsum(
            "qhd,khd->hqk",
            heads_view(query_group),
            heads_view(key_rows),
            preferred_element_type=jnp.float32,
        )
        * inv_root
    )
    prob_far = jnp.exp(scores_far - lse_group.T[:, :, None])
    grad_v = jnp.einsum(
        "hqk,qhd->khd",
        prob_far.astype(jnp.bfloat16),
        heads_view(grad_group),
        preferred_element_type=jnp.float32,
    )
    dprob_far = jnp.einsum(
        "qhd,khd->hqk",
        heads_view(grad_group),
        heads_view(value_rows),
        preferred_element_type=jnp.float32,
    )
    dscore_far = (prob_far * (dprob_far - offset_group.T[:, :, None])).astype(jnp.bfloat16)
    grad_k = (
        jnp.einsum(
            "hqk,qhd->khd", dscore_far, heads_view(query_group), preferred_element_type=jnp.float32
        )
        * inv_root
    )
    return grad_k, grad_v


def on_device(query_states, key_states, value_states, out_proj, grad_output):
    queries = query_states[0]
    keys_all = key_states[0]
    values_all = value_states[0]
    upstream = grad_output[0]
    row_count = queries.shape[0]
    features = queries.shape[1]
    inv_root = HD ** (-0.5)
    devices = lax.axis_size("tm")
    bit_count = devices.bit_length() - 1
    top_bit = bit_count - 1
    near_first = {0: 3, 1: 1, 2: 0, 3: 4, 4: 2, 5: 5}
    low_bits = sorted(range(top_bit), key=lambda b: near_first.get(b, b))
    wide = features + 128

    qkv = jnp.stack([by_parity(pick_rows(m, R2)) for m in (queries, keys_all, values_all)], 0)
    per_par = qkv.shape[2]
    own, other_qkv = gather_with_rider(
        qkv[:, :, None], 2, low_bits, jnp.stack([queries, keys_all, values_all], 0)
    )
    far = partner(own[:, 0], "tm", top_bit)
    other_q = other_qkv[0]
    keys_one = jnp.concatenate([keys_all, other_qkv[1]], 0)
    values_one = jnp.concatenate([values_all, other_qkv[2]], 0)
    part_one, lse_one = attend(queries, keys_one, values_one, inv_root)
    q_seg2 = own[0].reshape(-1, features)
    k_seg2 = own[1].reshape(-1, features)
    v_seg2 = own[2].reshape(-1, features)
    q_seg3 = jnp.concatenate([own[0, 0], far[0]], 0).reshape(-1, features)
    k_seg3 = jnp.concatenate([own[1, 0], far[1]], 0).reshape(-1, features)
    v_seg3 = jnp.concatenate([own[2, 0], far[2]], 0).reshape(-1, features)
    q_two = qkv[0].reshape(-1, features)
    q_three = qkv[0, 0]
    part_two, lse_two = attend(q_two, k_seg2, v_seg2, inv_root)
    part_three, lse_three = attend(q_three, k_seg3, v_seg3, inv_root)

    partials = [
        spread_rows(part_one, 1),
        spread_rows(from_parity(part_two.reshape((2, per_par) + part_two.shape[1:])), R2),
        spread_rows(part_three, R3),
    ]
    log_totals = [
        spread_stats(lse_one, 1),
        spread_stats(from_parity(lse_two.reshape(2, per_par, HEADS)), R2),
        spread_stats(lse_three, R3),
    ]
    coverage = [cover_table(row_count, d) for d in (1, R2, R3)]
    merged, weights = merge_levels(log_totals, coverage, partials)
    attn = merged.reshape(row_count, features).astype(jnp.bfloat16)
    output = jnp.dot(attn, out_proj, preferred_element_type=jnp.float32).astype(jnp.bfloat16)
    grad_attn = lax.dot_general(
        upstream, out_proj, (((1,), (1,)), ((), ())), preferred_element_type=jnp.float32
    ).astype(jnp.bfloat16)
    proj_part = lax.dot_general(
        attn, upstream, (((0,), (0,)), ((), ())), preferred_element_type=jnp.float32
    )
    order = (0, 2, 5, 7, 3, 6, 8, 4, 1)
    grad_proj = scatter_sum(proj_part, ("tm", "batch"), order)

    grad_three = grad_attn.astype(jnp.float32).reshape(row_count, HEADS, HD)
    rowdot = jnp.sum(grad_three * merged, axis=2)

    def grad_of(weight_now, grad_rows):
        scaled = weight_now[:, :, None] * grad_rows.astype(jnp.float32).reshape(-1, HEADS, HD)
        return scaled.astype(jnp.bfloat16).reshape(-1, features)

    grad_one = grad_of(weights[0], grad_attn)
    offset_one = weights[0] * rowdot
    packed_one = jnp.concatenate([grad_one, split_exact(jnp.concatenate([lse_one, offset_one], 1))], 1)

    ga_par = by_parity(pick_rows(grad_attn, R2))
    w_two = by_parity(pick_stats(weights[1], R2))
    rd_two = by_parity(pick_stats(rowdot, R2))
    lse_two_par = lse_two.reshape(2, per_par, HEADS)
    w_three = pick_stats(weights[2], R3)
    no_level = jnp.zeros_like(w_three)
    lse3_par = jnp.stack([lse_three, no_level], 0)
    w3_par = jnp.stack([w_three, no_level], 0)
    stats_par = jnp.concatenate([lse_two_par, w_two, lse3_par, w3_par, rd_two], -1)
    packed = pad_lanes(jnp.concatenate([ga_par, split_exact(stats_par)], -1), wide)
    own_b, other_one = gather_with_rider(packed[:, None], 1, low_bits, pad_lanes(packed_one, wide))
    other_stats = join_exact(other_one[:, features : features + 6 * HEADS])
    total_q = spread_rows(
        near_grad(queries, keys_one, values_one, grad_one, lse_one, offset_one, inv_root), 1
    )
    k_g1, v_g1 = far_grad(
        jnp.concatenate([queries, other_q], 0),
        jnp.concatenate([grad_one, other_one[:, :features]], 0),
        jnp.concatenate([lse_one, other_stats[:, :HEADS]], 0),
        jnp.concatenate([offset_one, other_stats[:, HEADS:]], 0),
        keys_all,
        values_all,
        inv_root,
    )
    total_k = spread_rows(k_g1, 1)
    total_v = spread_rows(v_g1, 1)
    far_b = partner(own_b[0], "tm", top_bit)
    stat_w = 5 * HEADS

    def unpack(rows):
        rows = rows.reshape(-1, wide)
        stats = join_exact(rows[:, features : features + 3 * stat_w])
        return rows[:, :features], stats.reshape(-1, 5, HEADS)

    g_two = grad_of(w_two.reshape(-1, HEADS), ga_par.reshape(-1, features))
    c_two = w_two.reshape(-1, HEADS) * rd_two.reshape(-1, HEADS)
    grad_q2 = near_grad(q_two, k_seg2, v_seg2, g_two, lse_two, c_two, inv_root)
    ga_seg2, st_seg2 = unpack(own_b)
    k_g2, v_g2 = far_grad(
        q_seg2,
        grad_of(st_seg2[:, 1], ga_seg2),
        st_seg2[:, 0],
        st_seg2[:, 1] * st_seg2[:, 4],
        qkv[1].reshape(-1, features),
        qkv[2].reshape(-1, features),
        inv_root,
    )

    g_three = grad_of(w_three, ga_par[0])
    c_three = w_three * rd_two[0]
    grad_q3 = near_grad(q_three, k_seg3, v_seg3, g_three, lse_three, c_three, inv_root)
    ga_seg3, st_seg3 = unpack(jnp.concatenate([own_b[0], far_b], 0))
    k_g3, v_g3 = far_grad(
        q_seg3,
        grad_of(st_seg3[:, 3], ga_seg3),
        st_seg3[:, 2],
        st_seg3[:, 3] * st_seg3[:, 4],
        qkv[1, 0],
        qkv[2, 0],
        inv_root,
    )

    def level_two_rows(values):
        return spread_rows(from_parity(values.reshape((2, per_par) + values.shape[1:])), R2)

    total_q = total_q + level_two_rows(grad_q2) + spread_rows(grad_q3, R3)
    total_k = total_k + level_two_rows(k_g2) + spread_rows(k_g3, R3)
    total_v = total_v + level_two_rows(v_g2) + spread_rows(v_g3, R3)
    grad_query = total_q.reshape(row_count, features).astype(jnp.bfloat16)
    grad_key = total_k.reshape(row_count, features).astype(jnp.bfloat16)
    grad_value = total_v.reshape(row_count, features).astype(jnp.bfloat16)
    return (output[None], grad_query[None], grad_key[None], grad_value[None], grad_proj)


def solution(mesh):
    in_specs = (
        P("batch", "tm", None),
        P("batch", "tm", None),
        P("batch", "tm", None),
        P(),
        P("batch", "tm", None),
    )
    out_specs = (
        P("batch", "tm", None),
        P("batch", "tm", None),
        P("batch", "tm", None),
        P("batch", "tm", None),
        P(("tm", "batch"), None),
    )
    return jax.shard_map(
        on_device, mesh=mesh, in_specs=in_specs, out_specs=out_specs, check_vma=False
    )
```

```python
import jax
import jax.numpy as jnp
import numpy as np
from jax import lax
from jax.sharding import PartitionSpec as P

HEADS = 8
HD = 64
R2 = 8
R3 = 16


def partner(value, axis, apart):
    mask = 2**apart
    pairs = [(source, source ^ mask) for source in range(lax.axis_size(axis))]
    return lax.ppermute(value, axis, pairs)


def offset_mask(dilation):
    return (np.arange(dilation)[:, None] == (np.arange(HEADS) % dilation)[None, :]).astype(
        np.float32
    )


def cover_table(row_count, dilation):
    return (np.arange(row_count) % dilation)[:, None] == (np.arange(HEADS) % dilation)[None, :]


def pick_rows(matrix, dilation):
    count = matrix.shape[0] // dilation
    blocks = matrix.reshape(count, dilation, HEADS, HD)
    chooser = jnp.asarray(offset_mask(dilation), matrix.dtype)[None, :, :, None]
    return jnp.sum(blocks * chooser, axis=1).reshape(count, HEADS * HD)


def pick_stats(matrix, dilation):
    count = matrix.shape[0] // dilation
    blocks = matrix.reshape(count, dilation, HEADS)
    chooser = jnp.asarray(offset_mask(dilation), matrix.dtype)[None, :, :]
    return jnp.sum(blocks * chooser, axis=1)


def spread_rows(values, dilation):
    chooser = jnp.asarray(offset_mask(dilation), values.dtype)[None, :, :, None]
    return (values[:, None] * chooser).reshape(values.shape[0] * dilation, HEADS, HD)


def spread_stats(values, dilation):
    chooser = jnp.asarray(offset_mask(dilation), values.dtype)[None, :, :]
    return (values[:, None] * chooser).reshape(values.shape[0] * dilation, HEADS)


def merge_levels(log_totals, coverage, partials):
    first_lse = log_totals[0]
    peak = first_lse
    for level_no in range(1, len(log_totals)):
        peak = jnp.maximum(peak, jnp.where(coverage[level_no], log_totals[level_no], first_lse))
    exponents = []
    for level_no in range(len(log_totals)):
        exponents.append(jnp.where(coverage[level_no], jnp.exp(log_totals[level_no] - peak), 0.0))
    denominator = exponents[0]
    for level_no in range(1, len(exponents)):
        denominator = denominator + exponents[level_no]
    weights = []
    merged = None
    for level_no in range(len(exponents)):
        weight_now = exponents[level_no] / denominator
        weights.append(weight_now)
        term = weight_now[:, :, None] * partials[level_no]
        merged = term if merged is None else merged + term
    return (merged, weights)


def gather_blocks(block, axis_pos, bit_order):
    for bit_pos in bit_order:
        block = jnp.concatenate([block, partner(block, "tm", bit_pos)], axis_pos)
    return block


def gather_with_rider(block, axis_pos, bit_order, rider):
    lanes = block.shape[-1]
    for bit_pos in bit_order:
        if bit_pos == 0:
            rows = block.size // lanes
            message = jnp.concatenate([block.reshape(rows, lanes), rider.reshape(-1, lanes)], 0)
            got = partner(message, "tm", bit_pos)
            other = got[:rows].reshape(block.shape)
            rider_back = got[rows:].reshape(rider.shape)
        else:
            other = partner(block, "tm", bit_pos)
        block = jnp.concatenate([block, other], axis_pos)
    return block, rider_back


def split_exact(values):
    high = lax.reduce_precision(values, exponent_bits=8, mantissa_bits=7)
    rest = values - high
    middle = lax.reduce_precision(rest, exponent_bits=8, mantissa_bits=7)
    low = rest - middle
    parts = jnp.concatenate([high, middle, low], -1)
    return parts.astype(jnp.bfloat16)


def join_exact(parts):
    width = parts.shape[-1] // 3
    as32 = parts.astype(jnp.float32)
    return as32[..., :width] + (as32[..., width : 2 * width] + as32[..., 2 * width :])


def by_parity(rows):
    return rows.reshape((rows.shape[0] // 2, 2) + rows.shape[1:]).swapaxes(0, 1)


def from_parity(rows):
    return rows.swapaxes(0, 1).reshape((rows.shape[0] * rows.shape[1],) + rows.shape[2:])


def pad_lanes(matrix, width):
    return jnp.pad(matrix, [(0, 0)] * (matrix.ndim - 1) + [(0, width - matrix.shape[-1])])


def scatter_sum(matrix, axes, bit_order):
    index = lax.axis_index(axes)
    bit_count = len(bit_order)
    size = 1 << bit_count
    block = matrix.reshape((2,) * bit_count + matrix.shape[1:])
    dims = [bit_count - 1 - j for j in range(bit_count)]
    for bit_pos in bit_order:
        axis_pos = dims.index(bit_pos)
        my_bit = index // (1 << bit_pos) % 2
        keep = lax.dynamic_index_in_dim(block, my_bit, axis_pos, keepdims=False)
        send = lax.dynamic_index_in_dim(block, 1 - my_bit, axis_pos, keepdims=False)
        pairs = [(source, source ^ (1 << bit_pos)) for source in range(size)]
        block = keep + lax.ppermute(send, axes, pairs)
        dims.pop(axis_pos)
    return block.reshape((1,) + matrix.shape[1:])


def heads_view(matrix):
    return matrix.reshape(matrix.shape[0], HEADS, HD)


def attend(query_rows, key_rows, value_rows, inv_root):
    scores = (
        jnp.einsum(
            "qhd,khd->hqk",
            heads_view(query_rows),
            heads_view(key_rows),
            preferred_element_type=jnp.float32,
        )
        * inv_root
    )
    peak = jnp.max(scores, axis=2, keepdims=True)
    log_total = peak + jnp.log(jnp.sum(jnp.exp(scores - peak), axis=2, keepdims=True))
    weights_bf = jnp.exp(scores - log_total).astype(jnp.bfloat16)
    part_out = jnp.einsum(
        "hqk,khd->qhd", weights_bf, heads_view(value_rows), preferred_element_type=jnp.float32
    )
    return part_out, log_total[:, :, 0].T


def near_grad(query_rows, key_rows, value_rows, grad_rows, lse_rows, offset_rows, inv_root):
    scores = (
        jnp.einsum(
            "qhd,khd->hqk",
            heads_view(query_rows),
            heads_view(key_rows),
            preferred_element_type=jnp.float32,
        )
        * inv_root
    )
    prob_full = jnp.exp(scores - lse_rows.T[:, :, None])
    dprob = jnp.einsum(
        "qhd,khd->hqk",
        heads_view(grad_rows),
        heads_view(value_rows),
        preferred_element_type=jnp.float32,
    )
    dscore = (prob_full * (dprob - offset_rows.T[:, :, None])).astype(jnp.bfloat16)
    return (
        jnp.einsum("hqk,khd->qhd", dscore, heads_view(key_rows), preferred_element_type=jnp.float32)
        * inv_root
    )


def far_grad(query_group, grad_group, lse_group, offset_group, key_rows, value_rows, inv_root):
    scores_far = (
        jnp.einsum(
            "qhd,khd->hqk",
            heads_view(query_group),
            heads_view(key_rows),
            preferred_element_type=jnp.float32,
        )
        * inv_root
    )
    prob_far = jnp.exp(scores_far - lse_group.T[:, :, None])
    grad_v = jnp.einsum(
        "hqk,qhd->khd",
        prob_far.astype(jnp.bfloat16),
        heads_view(grad_group),
        preferred_element_type=jnp.float32,
    )
    dprob_far = jnp.einsum(
        "qhd,khd->hqk",
        heads_view(grad_group),
        heads_view(value_rows),
        preferred_element_type=jnp.float32,
    )
    dscore_far = (prob_far * (dprob_far - offset_group.T[:, :, None])).astype(jnp.bfloat16)
    grad_k = (
        jnp.einsum(
            "hqk,qhd->khd", dscore_far, heads_view(query_group), preferred_element_type=jnp.float32
        )
        * inv_root
    )
    return grad_k, grad_v


def on_device(query_states, key_states, value_states, out_proj, grad_output):
    queries = query_states[0]
    keys_all = key_states[0]
    values_all = value_states[0]
    upstream = grad_output[0]
    row_count = queries.shape[0]
    features = queries.shape[1]
    inv_root = HD ** (-0.5)
    devices = lax.axis_size("tm")
    bit_count = devices.bit_length() - 1
    top_bit = bit_count - 1
    near_first = {0: 3, 1: 1, 2: 0, 3: 4, 4: 2, 5: 5}
    low_bits = sorted(range(top_bit), key=lambda b: near_first.get(b, b))
    wide = features + 128

    qkv = jnp.stack([by_parity(pick_rows(m, R2)) for m in (queries, keys_all, values_all)], 0)
    per_par = qkv.shape[2]
    far = partner(qkv[:, 0], "tm", top_bit)
    own, other_qkv = gather_with_rider(
        jnp.concatenate([qkv, far[:, None]], 1)[:, :, None],
        2,
        low_bits,
        jnp.stack([queries, keys_all, values_all], 0),
    )
    other_q = other_qkv[0]
    keys_one = jnp.concatenate([keys_all, other_qkv[1]], 0)
    values_one = jnp.concatenate([values_all, other_qkv[2]], 0)
    part_one, lse_one = attend(queries, keys_one, values_one, inv_root)
    q_seg2 = own[0, :2].reshape(-1, features)
    k_seg2 = own[1, :2].reshape(-1, features)
    v_seg2 = own[2, :2].reshape(-1, features)
    q_seg3 = own[0, ::2].reshape(-1, features)
    k_seg3 = own[1, ::2].reshape(-1, features)
    v_seg3 = own[2, ::2].reshape(-1, features)
    q_two = qkv[0].reshape(-1, features)
    q_three = qkv[0, 0]
    part_two, lse_two = attend(q_two, k_seg2, v_seg2, inv_root)
    part_three, lse_three = attend(q_three, k_seg3, v_seg3, inv_root)

    partials = [
        spread_rows(part_one, 1),
        spread_rows(from_parity(part_two.reshape((2, per_par) + part_two.shape[1:])), R2),
        spread_rows(part_three, R3),
    ]
    log_totals = [
        spread_stats(lse_one, 1),
        spread_stats(from_parity(lse_two.reshape(2, per_par, HEADS)), R2),
        spread_stats(lse_three, R3),
    ]
    coverage = [cover_table(row_count, d) for d in (1, R2, R3)]
    merged, weights = merge_levels(log_totals, coverage, partials)
    attn = merged.reshape(row_count, features).astype(jnp.bfloat16)
    output = jnp.dot(attn, out_proj, preferred_element_type=jnp.float32).astype(jnp.bfloat16)
    grad_attn = lax.dot_general(
        upstream, out_proj, (((1,), (1,)), ((), ())), preferred_element_type=jnp.float32
    ).astype(jnp.bfloat16)
    proj_part = lax.dot_general(
        attn, upstream, (((0,), (0,)), ((), ())), preferred_element_type=jnp.float32
    )
    order = (0, 2, 5, 7, 3, 6, 8, 4, 1)
    grad_proj = scatter_sum(proj_part, ("tm", "batch"), order)

    grad_three = grad_attn.astype(jnp.float32).reshape(row_count, HEADS, HD)
    rowdot = jnp.sum(grad_three * merged, axis=2)

    def grad_of(weight_now, grad_rows):
        scaled = weight_now[:, :, None] * grad_rows.astype(jnp.float32).reshape(-1, HEADS, HD)
        return scaled.astype(jnp.bfloat16).reshape(-1, features)

    grad_one = grad_of(weights[0], grad_attn)
    offset_one = weights[0] * rowdot
    packed_one = jnp.concatenate([grad_one, split_exact(jnp.concatenate([lse_one, offset_one], 1))], 1)

    ga_par = by_parity(pick_rows(grad_attn, R2))
    w_two = by_parity(pick_stats(weights[1], R2))
    rd_two = by_parity(pick_stats(rowdot, R2))
    lse_two_par = lse_two.reshape(2, per_par, HEADS)
    w_three = pick_stats(weights[2], R3)
    no_level = jnp.zeros_like(w_three)
    lse3_par = jnp.stack([lse_three, no_level], 0)
    w3_par = jnp.stack([w_three, no_level], 0)
    stats_par = jnp.concatenate([lse_two_par, w_two, lse3_par, w3_par, rd_two], -1)
    packed = pad_lanes(jnp.concatenate([ga_par, split_exact(stats_par)], -1), wide)
    far_b = partner(packed[0], "tm", top_bit)
    own_b, other_one = gather_with_rider(
        jnp.concatenate([packed, far_b[None]], 0)[:, None], 1, low_bits, pad_lanes(packed_one, wide)
    )
    other_stats = join_exact(other_one[:, features : features + 6 * HEADS])
    total_q = spread_rows(
        near_grad(queries, keys_one, values_one, grad_one, lse_one, offset_one, inv_root), 1
    )
    k_g1, v_g1 = far_grad(
        jnp.concatenate([queries, other_q], 0),
        jnp.concatenate([grad_one, other_one[:, :features]], 0),
        jnp.concatenate([lse_one, other_stats[:, :HEADS]], 0),
        jnp.concatenate([offset_one, other_stats[:, HEADS:]], 0),
        keys_all,
        values_all,
        inv_root,
    )
    total_k = spread_rows(k_g1, 1)
    total_v = spread_rows(v_g1, 1)
    stat_w = 5 * HEADS

    def unpack(rows):
        rows = rows.reshape(-1, wide)
        stats = join_exact(rows[:, features : features + 3 * stat_w])
        return rows[:, :features], stats.reshape(-1, 5, HEADS)

    g_two = grad_of(w_two.reshape(-1, HEADS), ga_par.reshape(-1, features))
    c_two = w_two.reshape(-1, HEADS) * rd_two.reshape(-1, HEADS)
    grad_q2 = near_grad(q_two, k_seg2, v_seg2, g_two, lse_two, c_two, inv_root)
    ga_seg2, st_seg2 = unpack(own_b[:2])
    k_g2, v_g2 = far_grad(
        q_seg2,
        grad_of(st_seg2[:, 1], ga_seg2),
        st_seg2[:, 0],
        st_seg2[:, 1] * st_seg2[:, 4],
        qkv[1].reshape(-1, features),
        qkv[2].reshape(-1, features),
        inv_root,
    )

    g_three = grad_of(w_three, ga_par[0])
    c_three = w_three * rd_two[0]
    grad_q3 = near_grad(q_three, k_seg3, v_seg3, g_three, lse_three, c_three, inv_root)
    ga_seg3, st_seg3 = unpack(own_b[::2])
    k_g3, v_g3 = far_grad(
        q_seg3,
        grad_of(st_seg3[:, 3], ga_seg3),
        st_seg3[:, 2],
        st_seg3[:, 3] * st_seg3[:, 4],
        qkv[1, 0],
        qkv[2, 0],
        inv_root,
    )

    def level_two_rows(values):
        return spread_rows(from_parity(values.reshape((2, per_par) + values.shape[1:])), R2)

    total_q = total_q + level_two_rows(grad_q2) + spread_rows(grad_q3, R3)
    total_k = total_k + level_two_rows(k_g2) + spread_rows(k_g3, R3)
    total_v = total_v + level_two_rows(v_g2) + spread_rows(v_g3, R3)
    grad_query = total_q.reshape(row_count, features).astype(jnp.bfloat16)
    grad_key = total_k.reshape(row_count, features).astype(jnp.bfloat16)
    grad_value = total_v.reshape(row_count, features).astype(jnp.bfloat16)
    return (output[None], grad_query[None], grad_key[None], grad_value[None], grad_proj)


def solution(mesh):
    in_specs = (
        P("batch", "tm", None),
        P("batch", "tm", None),
        P("batch", "tm", None),
        P(),
        P("batch", "tm", None),
    )
    out_specs = (
        P("batch", "tm", None),
        P("batch", "tm", None),
        P("batch", "tm", None),
        P("batch", "tm", None),
        P(("tm", "batch"), None),
    )
    return jax.shard_map(
        on_device, mesh=mesh, in_specs=in_specs, out_specs=out_specs, check_vma=False
    )
```

```python
import jax
import jax.numpy as jnp
import numpy as np
from jax import lax
from jax.sharding import PartitionSpec as P

HEADS = 8
HD = 64
R2 = 8
R3 = 16


def partner(value, axis, apart):
    mask = 2**apart
    pairs = [(source, source ^ mask) for source in range(lax.axis_size(axis))]
    return lax.ppermute(value, axis, pairs)


def offset_mask(dilation):
    return (np.arange(dilation)[:, None] == (np.arange(HEADS) % dilation)[None, :]).astype(
        np.float32
    )


def cover_table(row_count, dilation):
    return (np.arange(row_count) % dilation)[:, None] == (np.arange(HEADS) % dilation)[None, :]


def pick_rows(matrix, dilation):
    count = matrix.shape[0] // dilation
    blocks = matrix.reshape(count, dilation, HEADS, HD)
    chooser = jnp.asarray(offset_mask(dilation), matrix.dtype)[None, :, :, None]
    return jnp.sum(blocks * chooser, axis=1).reshape(count, HEADS * HD)


def pick_stats(matrix, dilation):
    count = matrix.shape[0] // dilation
    blocks = matrix.reshape(count, dilation, HEADS)
    chooser = jnp.asarray(offset_mask(dilation), matrix.dtype)[None, :, :]
    return jnp.sum(blocks * chooser, axis=1)


def spread_rows(values, dilation):
    chooser = jnp.asarray(offset_mask(dilation), values.dtype)[None, :, :, None]
    return (values[:, None] * chooser).reshape(values.shape[0] * dilation, HEADS, HD)


def spread_stats(values, dilation):
    chooser = jnp.asarray(offset_mask(dilation), values.dtype)[None, :, :]
    return (values[:, None] * chooser).reshape(values.shape[0] * dilation, HEADS)


def merge_levels(log_totals, coverage, partials):
    first_lse = log_totals[0]
    peak = first_lse
    for level_no in range(1, len(log_totals)):
        peak = jnp.maximum(peak, jnp.where(coverage[level_no], log_totals[level_no], first_lse))
    exponents = []
    for level_no in range(len(log_totals)):
        exponents.append(jnp.where(coverage[level_no], jnp.exp(log_totals[level_no] - peak), 0.0))
    denominator = exponents[0]
    for level_no in range(1, len(exponents)):
        denominator = denominator + exponents[level_no]
    weights = []
    merged = None
    for level_no in range(len(exponents)):
        weight_now = exponents[level_no] / denominator
        weights.append(weight_now)
        term = weight_now[:, :, None] * partials[level_no]
        merged = term if merged is None else merged + term
    return (merged, weights)


def gather_blocks(block, axis_pos, bit_order):
    for bit_pos in bit_order:
        block = jnp.concatenate([block, partner(block, "tm", bit_pos)], axis_pos)
    return block


def gather_with_rider(block, axis_pos, bit_order, rider):
    lanes = block.shape[-1]
    for bit_pos in bit_order:
        if bit_pos == 0:
            rows = block.size // lanes
            message = jnp.concatenate([block.reshape(rows, lanes), rider.reshape(-1, lanes)], 0)
            got = partner(message, "tm", bit_pos)
            other = got[:rows].reshape(block.shape)
            rider_back = got[rows:].reshape(rider.shape)
        else:
            other = partner(block, "tm", bit_pos)
        block = jnp.concatenate([block, other], axis_pos)
    return block, rider_back


def split_exact(values):
    high = lax.reduce_precision(values, exponent_bits=8, mantissa_bits=7)
    rest = values - high
    middle = lax.reduce_precision(rest, exponent_bits=8, mantissa_bits=7)
    low = rest - middle
    parts = jnp.concatenate([high, middle, low], -1)
    return parts.astype(jnp.bfloat16)


def join_exact(parts):
    width = parts.shape[-1] // 3
    as32 = parts.astype(jnp.float32)
    return as32[..., :width] + (as32[..., width : 2 * width] + as32[..., 2 * width :])


def by_parity(rows):
    return rows.reshape((rows.shape[0] // 2, 2) + rows.shape[1:]).swapaxes(0, 1)


def from_parity(rows):
    return rows.swapaxes(0, 1).reshape((rows.shape[0] * rows.shape[1],) + rows.shape[2:])


def pad_lanes(matrix, width):
    return jnp.pad(matrix, [(0, 0)] * (matrix.ndim - 1) + [(0, width - matrix.shape[-1])])


def scatter_sum(matrix, axes, bit_order):
    index = lax.axis_index(axes)
    bit_count = len(bit_order)
    size = 1 << bit_count
    block = matrix.reshape((2,) * bit_count + matrix.shape[1:])
    dims = [bit_count - 1 - j for j in range(bit_count)]
    for bit_pos in bit_order:
        axis_pos = dims.index(bit_pos)
        my_bit = index // (1 << bit_pos) % 2
        keep = lax.dynamic_index_in_dim(block, my_bit, axis_pos, keepdims=False)
        send = lax.dynamic_index_in_dim(block, 1 - my_bit, axis_pos, keepdims=False)
        pairs = [(source, source ^ (1 << bit_pos)) for source in range(size)]
        block = keep + lax.ppermute(send, axes, pairs)
        dims.pop(axis_pos)
    return block.reshape((1,) + matrix.shape[1:])


def heads_view(matrix):
    return matrix.reshape(matrix.shape[0], HEADS, HD)


def attend(query_rows, key_rows, value_rows, inv_root):
    scores = (
        jnp.einsum(
            "qhd,khd->hqk",
            heads_view(query_rows),
            heads_view(key_rows),
            preferred_element_type=jnp.float32,
        )
        * inv_root
    )
    peak = jnp.max(scores, axis=2, keepdims=True)
    log_total = peak + jnp.log(jnp.sum(jnp.exp(scores - peak), axis=2, keepdims=True))
    weights_bf = jnp.exp(scores - log_total).astype(jnp.bfloat16)
    part_out = jnp.einsum(
        "hqk,khd->qhd", weights_bf, heads_view(value_rows), preferred_element_type=jnp.float32
    )
    return part_out, log_total[:, :, 0].T


def near_grad(query_rows, key_rows, value_rows, grad_rows, lse_rows, offset_rows, inv_root):
    scores = (
        jnp.einsum(
            "qhd,khd->hqk",
            heads_view(query_rows),
            heads_view(key_rows),
            preferred_element_type=jnp.float32,
        )
        * inv_root
    )
    prob_full = jnp.exp(scores - lse_rows.T[:, :, None])
    dprob = jnp.einsum(
        "qhd,khd->hqk",
        heads_view(grad_rows),
        heads_view(value_rows),
        preferred_element_type=jnp.float32,
    )
    dscore = (prob_full * (dprob - offset_rows.T[:, :, None])).astype(jnp.bfloat16)
    return (
        jnp.einsum("hqk,khd->qhd", dscore, heads_view(key_rows), preferred_element_type=jnp.float32)
        * inv_root
    )


def far_grad(query_group, grad_group, lse_group, offset_group, key_rows, value_rows, inv_root):
    scores_far = (
        jnp.einsum(
            "qhd,khd->hqk",
            heads_view(query_group),
            heads_view(key_rows),
            preferred_element_type=jnp.float32,
        )
        * inv_root
    )
    prob_far = jnp.exp(scores_far - lse_group.T[:, :, None])
    grad_v = jnp.einsum(
        "hqk,qhd->khd",
        prob_far.astype(jnp.bfloat16),
        heads_view(grad_group),
        preferred_element_type=jnp.float32,
    )
    dprob_far = jnp.einsum(
        "qhd,khd->hqk",
        heads_view(grad_group),
        heads_view(value_rows),
        preferred_element_type=jnp.float32,
    )
    dscore_far = (prob_far * (dprob_far - offset_group.T[:, :, None])).astype(jnp.bfloat16)
    grad_k = (
        jnp.einsum(
            "hqk,qhd->khd", dscore_far, heads_view(query_group), preferred_element_type=jnp.float32
        )
        * inv_root
    )
    return grad_k, grad_v


def on_device(query_states, key_states, value_states, out_proj, grad_output):
    queries = query_states[0]
    keys_all = key_states[0]
    values_all = value_states[0]
    upstream = grad_output[0]
    row_count = queries.shape[0]
    features = queries.shape[1]
    inv_root = HD ** (-0.5)
    devices = lax.axis_size("tm")
    bit_count = devices.bit_length() - 1
    top_bit = bit_count - 1
    near_first = {0: 1, 1: 2, 2: 0, 3: 4, 4: 3, 5: 5}
    low_bits = sorted(range(top_bit), key=lambda b: near_first.get(b, b))
    wide = features + 128

    qkv = jnp.stack([by_parity(pick_rows(m, R2)) for m in (queries, keys_all, values_all)], 0)
    per_par = qkv.shape[2]
    own, other_qkv = gather_with_rider(
        qkv[:, :, None], 2, low_bits, jnp.stack([queries, keys_all, values_all], 0)
    )
    far = partner(own[:, 0], "tm", top_bit)
    other_q = other_qkv[0]
    keys_one = jnp.concatenate([keys_all, other_qkv[1]], 0)
    values_one = jnp.concatenate([values_all, other_qkv[2]], 0)
    part_one, lse_one = attend(queries, keys_one, values_one, inv_root)
    q_seg2 = own[0].reshape(-1, features)
    k_seg2 = own[1].reshape(-1, features)
    v_seg2 = own[2].reshape(-1, features)
    q_seg3 = jnp.concatenate([own[0, 0], far[0]], 0).reshape(-1, features)
    k_seg3 = jnp.concatenate([own[1, 0], far[1]], 0).reshape(-1, features)
    v_seg3 = jnp.concatenate([own[2, 0], far[2]], 0).reshape(-1, features)
    q_two = qkv[0].reshape(-1, features)
    q_three = qkv[0, 0]
    part_two, lse_two = attend(q_two, k_seg2, v_seg2, inv_root)
    part_three, lse_three = attend(q_three, k_seg3, v_seg3, inv_root)

    partials = [
        spread_rows(part_one, 1),
        spread_rows(from_parity(part_two.reshape((2, per_par) + part_two.shape[1:])), R2),
        spread_rows(part_three, R3),
    ]
    log_totals = [
        spread_stats(lse_one, 1),
        spread_stats(from_parity(lse_two.reshape(2, per_par, HEADS)), R2),
        spread_stats(lse_three, R3),
    ]
    coverage = [cover_table(row_count, d) for d in (1, R2, R3)]
    merged, weights = merge_levels(log_totals, coverage, partials)
    attn = merged.reshape(row_count, features).astype(jnp.bfloat16)
    output = jnp.dot(attn, out_proj, preferred_element_type=jnp.float32).astype(jnp.bfloat16)
    grad_attn = lax.dot_general(
        upstream, out_proj, (((1,), (1,)), ((), ())), preferred_element_type=jnp.float32
    ).astype(jnp.bfloat16)
    proj_part = lax.dot_general(
        attn, upstream, (((0,), (0,)), ((), ())), preferred_element_type=jnp.float32
    )
    order = (0, 2, 5, 7, 3, 6, 8, 4, 1)
    grad_proj = scatter_sum(proj_part, ("tm", "batch"), order)

    grad_three = grad_attn.astype(jnp.float32).reshape(row_count, HEADS, HD)
    rowdot = jnp.sum(grad_three * merged, axis=2)

    def grad_of(weight_now, grad_rows):
        scaled = weight_now[:, :, None] * grad_rows.astype(jnp.float32).reshape(-1, HEADS, HD)
        return scaled.astype(jnp.bfloat16).reshape(-1, features)

    grad_one = grad_of(weights[0], grad_attn)
    offset_one = weights[0] * rowdot
    packed_one = jnp.concatenate([grad_one, split_exact(jnp.concatenate([lse_one, offset_one], 1))], 1)

    ga_par = by_parity(pick_rows(grad_attn, R2))
    w_two = by_parity(pick_stats(weights[1], R2))
    rd_two = by_parity(pick_stats(rowdot, R2))
    lse_two_par = lse_two.reshape(2, per_par, HEADS)
    w_three = pick_stats(weights[2], R3)
    no_level = jnp.zeros_like(w_three)
    lse3_par = jnp.stack([lse_three, no_level], 0)
    w3_par = jnp.stack([w_three, no_level], 0)
    stats_par = jnp.concatenate([lse_two_par, w_two, lse3_par, w3_par, rd_two], -1)
    packed = pad_lanes(jnp.concatenate([ga_par, split_exact(stats_par)], -1), wide)
    own_b, other_one = gather_with_rider(packed[:, None], 1, low_bits, pad_lanes(packed_one, wide))
    other_stats = join_exact(other_one[:, features : features + 6 * HEADS])
    total_q = spread_rows(
        near_grad(queries, keys_one, values_one, grad_one, lse_one, offset_one, inv_root), 1
    )
    k_g1, v_g1 = far_grad(
        jnp.concatenate([queries, other_q], 0),
        jnp.concatenate([grad_one, other_one[:, :features]], 0),
        jnp.concatenate([lse_one, other_stats[:, :HEADS]], 0),
        jnp.concatenate([offset_one, other_stats[:, HEADS:]], 0),
        keys_all,
        values_all,
        inv_root,
    )
    total_k = spread_rows(k_g1, 1)
    total_v = spread_rows(v_g1, 1)
    far_b = partner(own_b[0], "tm", top_bit)
    stat_w = 5 * HEADS

    def unpack(rows):
        rows = rows.reshape(-1, wide)
        stats = join_exact(rows[:, features : features + 3 * stat_w])
        return rows[:, :features], stats.reshape(-1, 5, HEADS)

    g_two = grad_of(w_two.reshape(-1, HEADS), ga_par.reshape(-1, features))
    c_two = w_two.reshape(-1, HEADS) * rd_two.reshape(-1, HEADS)
    grad_q2 = near_grad(q_two, k_seg2, v_seg2, g_two, lse_two, c_two, inv_root)
    ga_seg2, st_seg2 = unpack(own_b)
    k_g2, v_g2 = far_grad(
        q_seg2,
        grad_of(st_seg2[:, 1], ga_seg2),
        st_seg2[:, 0],
        st_seg2[:, 1] * st_seg2[:, 4],
        qkv[1].reshape(-1, features),
        qkv[2].reshape(-1, features),
        inv_root,
    )

    g_three = grad_of(w_three, ga_par[0])
    c_three = w_three * rd_two[0]
    grad_q3 = near_grad(q_three, k_seg3, v_seg3, g_three, lse_three, c_three, inv_root)
    ga_seg3, st_seg3 = unpack(jnp.concatenate([own_b[0], far_b], 0))
    k_g3, v_g3 = far_grad(
        q_seg3,
        grad_of(st_seg3[:, 3], ga_seg3),
        st_seg3[:, 2],
        st_seg3[:, 3] * st_seg3[:, 4],
        qkv[1, 0],
        qkv[2, 0],
        inv_root,
    )

    def level_two_rows(values):
        return spread_rows(from_parity(values.reshape((2, per_par) + values.shape[1:])), R2)

    total_q = total_q + level_two_rows(grad_q2) + spread_rows(grad_q3, R3)
    total_k = total_k + level_two_rows(k_g2) + spread_rows(k_g3, R3)
    total_v = total_v + level_two_rows(v_g2) + spread_rows(v_g3, R3)
    grad_query = total_q.reshape(row_count, features).astype(jnp.bfloat16)
    grad_key = total_k.reshape(row_count, features).astype(jnp.bfloat16)
    grad_value = total_v.reshape(row_count, features).astype(jnp.bfloat16)
    return (output[None], grad_query[None], grad_key[None], grad_value[None], grad_proj)


def solution(mesh):
    in_specs = (
        P("batch", "tm", None),
        P("batch", "tm", None),
        P("batch", "tm", None),
        P(),
        P("batch", "tm", None),
    )
    out_specs = (
        P("batch", "tm", None),
        P("batch", "tm", None),
        P("batch", "tm", None),
        P("batch", "tm", None),
        P(("tm", "batch"), None),
    )
    return jax.shard_map(
        on_device, mesh=mesh, in_specs=in_specs, out_specs=out_specs, check_vma=False
    )
```

```python
import jax
import jax.numpy as jnp
import numpy as np
from jax import lax
from jax.sharding import PartitionSpec as P

HEADS = 8
HD = 64
R2 = 8
R3 = 16


def partner(value, axis, apart):
    mask = 2**apart
    pairs = [(source, source ^ mask) for source in range(lax.axis_size(axis))]
    return lax.ppermute(value, axis, pairs)


def offset_mask(dilation):
    return (np.arange(dilation)[:, None] == (np.arange(HEADS) % dilation)[None, :]).astype(
        np.float32
    )


def cover_table(row_count, dilation):
    return (np.arange(row_count) % dilation)[:, None] == (np.arange(HEADS) % dilation)[None, :]


def pick_rows(matrix, dilation):
    count = matrix.shape[0] // dilation
    blocks = matrix.reshape(count, dilation, HEADS, HD)
    chooser = jnp.asarray(offset_mask(dilation), matrix.dtype)[None, :, :, None]
    return jnp.sum(blocks * chooser, axis=1).reshape(count, HEADS * HD)


def pick_stats(matrix, dilation):
    count = matrix.shape[0] // dilation
    blocks = matrix.reshape(count, dilation, HEADS)
    chooser = jnp.asarray(offset_mask(dilation), matrix.dtype)[None, :, :]
    return jnp.sum(blocks * chooser, axis=1)


def spread_rows(values, dilation):
    chooser = jnp.asarray(offset_mask(dilation), values.dtype)[None, :, :, None]
    return (values[:, None] * chooser).reshape(values.shape[0] * dilation, HEADS, HD)


def spread_stats(values, dilation):
    chooser = jnp.asarray(offset_mask(dilation), values.dtype)[None, :, :]
    return (values[:, None] * chooser).reshape(values.shape[0] * dilation, HEADS)


def merge_levels(log_totals, coverage, partials):
    first_lse = log_totals[0]
    peak = first_lse
    for level_no in range(1, len(log_totals)):
        peak = jnp.maximum(peak, jnp.where(coverage[level_no], log_totals[level_no], first_lse))
    exponents = []
    for level_no in range(len(log_totals)):
        exponents.append(jnp.where(coverage[level_no], jnp.exp(log_totals[level_no] - peak), 0.0))
    denominator = exponents[0]
    for level_no in range(1, len(exponents)):
        denominator = denominator + exponents[level_no]
    weights = []
    merged = None
    for level_no in range(len(exponents)):
        weight_now = exponents[level_no] / denominator
        weights.append(weight_now)
        term = weight_now[:, :, None] * partials[level_no]
        merged = term if merged is None else merged + term
    return (merged, weights)


def gather_blocks(block, axis_pos, bit_order):
    for bit_pos in bit_order:
        block = jnp.concatenate([block, partner(block, "tm", bit_pos)], axis_pos)
    return block


def gather_with_rider(block, axis_pos, bit_order, rider):
    lanes = block.shape[-1]
    for bit_pos in bit_order:
        if bit_pos == 0:
            rows = block.size // lanes
            message = jnp.concatenate([block.reshape(rows, lanes), rider.reshape(-1, lanes)], 0)
            got = partner(message, "tm", bit_pos)
            other = got[:rows].reshape(block.shape)
            rider_back = got[rows:].reshape(rider.shape)
        else:
            other = partner(block, "tm", bit_pos)
        block = jnp.concatenate([block, other], axis_pos)
    return block, rider_back


def split_exact(values):
    high = lax.reduce_precision(values, exponent_bits=8, mantissa_bits=7)
    rest = values - high
    middle = lax.reduce_precision(rest, exponent_bits=8, mantissa_bits=7)
    low = rest - middle
    parts = jnp.concatenate([high, middle, low], -1)
    return parts.astype(jnp.bfloat16)


def join_exact(parts):
    width = parts.shape[-1] // 3
    as32 = parts.astype(jnp.float32)
    return as32[..., :width] + (as32[..., width : 2 * width] + as32[..., 2 * width :])


def by_parity(rows):
    return rows.reshape((rows.shape[0] // 2, 2) + rows.shape[1:]).swapaxes(0, 1)


def from_parity(rows):
    return rows.swapaxes(0, 1).reshape((rows.shape[0] * rows.shape[1],) + rows.shape[2:])


def pad_lanes(matrix, width):
    return jnp.pad(matrix, [(0, 0)] * (matrix.ndim - 1) + [(0, width - matrix.shape[-1])])


def scatter_sum(matrix, axes, bit_order):
    index = lax.axis_index(axes)
    bit_count = len(bit_order)
    size = 1 << bit_count
    block = matrix.reshape((2,) * bit_count + matrix.shape[1:])
    dims = [bit_count - 1 - j for j in range(bit_count)]
    for bit_pos in bit_order:
        axis_pos = dims.index(bit_pos)
        my_bit = index // (1 << bit_pos) % 2
        keep = lax.dynamic_index_in_dim(block, my_bit, axis_pos, keepdims=False)
        send = lax.dynamic_index_in_dim(block, 1 - my_bit, axis_pos, keepdims=False)
        pairs = [(source, source ^ (1 << bit_pos)) for source in range(size)]
        block = keep + lax.ppermute(send, axes, pairs)
        dims.pop(axis_pos)
    return block.reshape((1,) + matrix.shape[1:])


def heads_view(matrix):
    return matrix.reshape(matrix.shape[0], HEADS, HD)


def attend(query_rows, key_rows, value_rows, inv_root):
    scores = (
        jnp.einsum(
            "qhd,khd->hqk",
            heads_view(query_rows),
            heads_view(key_rows),
            preferred_element_type=jnp.float32,
        )
        * inv_root
    )
    peak = jnp.max(scores, axis=2, keepdims=True)
    log_total = peak + jnp.log(jnp.sum(jnp.exp(scores - peak), axis=2, keepdims=True))
    weights_bf = jnp.exp(scores - log_total).astype(jnp.bfloat16)
    part_out = jnp.einsum(
        "hqk,khd->qhd", weights_bf, heads_view(value_rows), preferred_element_type=jnp.float32
    )
    return part_out, log_total[:, :, 0].T


def near_grad(query_rows, key_rows, value_rows, grad_rows, lse_rows, offset_rows, inv_root):
    scores = (
        jnp.einsum(
            "qhd,khd->hqk",
            heads_view(query_rows),
            heads_view(key_rows),
            preferred_element_type=jnp.float32,
        )
        * inv_root
    )
    prob_full = jnp.exp(scores - lse_rows.T[:, :, None])
    dprob = jnp.einsum(
        "qhd,khd->hqk",
        heads_view(grad_rows),
        heads_view(value_rows),
        preferred_element_type=jnp.float32,
    )
    dscore = (prob_full * (dprob - offset_rows.T[:, :, None])).astype(jnp.bfloat16)
    return (
        jnp.einsum("hqk,khd->qhd", dscore, heads_view(key_rows), preferred_element_type=jnp.float32)
        * inv_root
    )


def far_grad(query_group, grad_group, lse_group, offset_group, key_rows, value_rows, inv_root):
    scores_far = (
        jnp.einsum(
            "qhd,khd->hqk",
            heads_view(query_group),
            heads_view(key_rows),
            preferred_element_type=jnp.float32,
        )
        * inv_root
    )
    prob_far = jnp.exp(scores_far - lse_group.T[:, :, None])
    grad_v = jnp.einsum(
        "hqk,qhd->khd",
        prob_far.astype(jnp.bfloat16),
        heads_view(grad_group),
        preferred_element_type=jnp.float32,
    )
    dprob_far = jnp.einsum(
        "qhd,khd->hqk",
        heads_view(grad_group),
        heads_view(value_rows),
        preferred_element_type=jnp.float32,
    )
    dscore_far = (prob_far * (dprob_far - offset_group.T[:, :, None])).astype(jnp.bfloat16)
    grad_k = (
        jnp.einsum(
            "hqk,qhd->khd", dscore_far, heads_view(query_group), preferred_element_type=jnp.float32
        )
        * inv_root
    )
    return grad_k, grad_v


def on_device(query_states, key_states, value_states, out_proj, grad_output):
    queries = query_states[0]
    keys_all = key_states[0]
    values_all = value_states[0]
    upstream = grad_output[0]
    row_count = queries.shape[0]
    features = queries.shape[1]
    inv_root = HD ** (-0.5)
    devices = lax.axis_size("tm")
    bit_count = devices.bit_length() - 1
    top_bit = bit_count - 1
    near_first = {0: 3, 1: 1, 2: 0, 3: 4, 4: 2, 5: 5}
    low_bits = sorted(range(top_bit), key=lambda b: near_first.get(b, b))
    wide = 2 * features + 128

    qkv = jnp.stack([by_parity(pick_rows(m, R2)) for m in (queries, keys_all, values_all)], 0)
    per_par = qkv.shape[2]
    own, other_kv = gather_with_rider(
        qkv[1:, :, None], 2, low_bits, jnp.stack([keys_all, values_all], 0)
    )
    far = partner(own[:, 0], "tm", top_bit)
    keys_one = jnp.concatenate([keys_all, other_kv[0]], 0)
    values_one = jnp.concatenate([values_all, other_kv[1]], 0)
    part_one, lse_one = attend(queries, keys_one, values_one, inv_root)
    k_seg2 = own[0].reshape(-1, features)
    v_seg2 = own[1].reshape(-1, features)
    k_seg3 = jnp.concatenate([own[0, 0], far[0]], 0).reshape(-1, features)
    v_seg3 = jnp.concatenate([own[1, 0], far[1]], 0).reshape(-1, features)
    q_two = qkv[0].reshape(-1, features)
    q_three = qkv[0, 0]
    part_two, lse_two = attend(q_two, k_seg2, v_seg2, inv_root)
    part_three, lse_three = attend(q_three, k_seg3, v_seg3, inv_root)

    partials = [
        spread_rows(part_one, 1),
        spread_rows(from_parity(part_two.reshape((2, per_par) + part_two.shape[1:])), R2),
        spread_rows(part_three, R3),
    ]
    log_totals = [
        spread_stats(lse_one, 1),
        spread_stats(from_parity(lse_two.reshape(2, per_par, HEADS)), R2),
        spread_stats(lse_three, R3),
    ]
    coverage = [cover_table(row_count, d) for d in (1, R2, R3)]
    merged, weights = merge_levels(log_totals, coverage, partials)
    attn = merged.reshape(row_count, features).astype(jnp.bfloat16)
    output = jnp.dot(attn, out_proj, preferred_element_type=jnp.float32).astype(jnp.bfloat16)
    grad_attn = lax.dot_general(
        upstream, out_proj, (((1,), (1,)), ((), ())), preferred_element_type=jnp.float32
    ).astype(jnp.bfloat16)
    proj_part = lax.dot_general(
        attn, upstream, (((0,), (0,)), ((), ())), preferred_element_type=jnp.float32
    )
    order = (0, 2, 5, 7, 3, 6, 8, 4, 1)
    grad_proj = scatter_sum(proj_part, ("tm", "batch"), order)

    grad_three = grad_attn.astype(jnp.float32).reshape(row_count, HEADS, HD)
    rowdot = jnp.sum(grad_three * merged, axis=2)

    def grad_of(weight_now, grad_rows):
        scaled = weight_now[:, :, None] * grad_rows.astype(jnp.float32).reshape(-1, HEADS, HD)
        return scaled.astype(jnp.bfloat16).reshape(-1, features)

    grad_one = grad_of(weights[0], grad_attn)
    offset_one = weights[0] * rowdot
    stats_one = split_exact(jnp.concatenate([lse_one, offset_one], 1))
    packed_one = jnp.concatenate([queries, grad_one, stats_one], 1)

    ga_par = by_parity(pick_rows(grad_attn, R2))
    w_two = by_parity(pick_stats(weights[1], R2))
    rd_two = by_parity(pick_stats(rowdot, R2))
    lse_two_par = lse_two.reshape(2, per_par, HEADS)
    w_three = pick_stats(weights[2], R3)
    no_level = jnp.zeros_like(w_three)
    lse3_par = jnp.stack([lse_three, no_level], 0)
    w3_par = jnp.stack([w_three, no_level], 0)
    stats_par = jnp.concatenate([lse_two_par, w_two, lse3_par, w3_par, rd_two], -1)
    packed = pad_lanes(jnp.concatenate([qkv[0], ga_par, split_exact(stats_par)], -1), wide)
    own_b, other_one = gather_with_rider(packed[:, None], 1, low_bits, pad_lanes(packed_one, wide))
    other_q = other_one[:, :features]
    other_stats = join_exact(other_one[:, 2 * features : 2 * features + 6 * HEADS])
    total_q = spread_rows(
        near_grad(queries, keys_one, values_one, grad_one, lse_one, offset_one, inv_root), 1
    )
    k_g1, v_g1 = far_grad(
        jnp.concatenate([queries, other_q], 0),
        jnp.concatenate([grad_one, other_one[:, features : 2 * features]], 0),
        jnp.concatenate([lse_one, other_stats[:, :HEADS]], 0),
        jnp.concatenate([offset_one, other_stats[:, HEADS:]], 0),
        keys_all,
        values_all,
        inv_root,
    )
    total_k = spread_rows(k_g1, 1)
    total_v = spread_rows(v_g1, 1)
    far_b = partner(own_b[0], "tm", top_bit)
    stat_w = 5 * HEADS

    def unpack(rows):
        rows = rows.reshape(-1, wide)
        stats = join_exact(rows[:, 2 * features : 2 * features + 3 * stat_w])
        return rows[:, :features], rows[:, features : 2 * features], stats.reshape(-1, 5, HEADS)

    g_two = grad_of(w_two.reshape(-1, HEADS), ga_par.reshape(-1, features))
    c_two = w_two.reshape(-1, HEADS) * rd_two.reshape(-1, HEADS)
    grad_q2 = near_grad(q_two, k_seg2, v_seg2, g_two, lse_two, c_two, inv_root)
    q_seg2, ga_seg2, st_seg2 = unpack(own_b)
    k_g2, v_g2 = far_grad(
        q_seg2,
        grad_of(st_seg2[:, 1], ga_seg2),
        st_seg2[:, 0],
        st_seg2[:, 1] * st_seg2[:, 4],
        qkv[1].reshape(-1, features),
        qkv[2].reshape(-1, features),
        inv_root,
    )

    g_three = grad_of(w_three, ga_par[0])
    c_three = w_three * rd_two[0]
    grad_q3 = near_grad(q_three, k_seg3, v_seg3, g_three, lse_three, c_three, inv_root)
    q_seg3, ga_seg3, st_seg3 = unpack(jnp.concatenate([own_b[0], far_b], 0))
    k_g3, v_g3 = far_grad(
        q_seg3,
        grad_of(st_seg3[:, 3], ga_seg3),
        st_seg3[:, 2],
        st_seg3[:, 3] * st_seg3[:, 4],
        qkv[1, 0],
        qkv[2, 0],
        inv_root,
    )

    def level_two_rows(values):
        return spread_rows(from_parity(values.reshape((2, per_par) + values.shape[1:])), R2)

    total_q = total_q + level_two_rows(grad_q2) + spread_rows(grad_q3, R3)
    total_k = total_k + level_two_rows(k_g2) + spread_rows(k_g3, R3)
    total_v = total_v + level_two_rows(v_g2) + spread_rows(v_g3, R3)
    grad_query = total_q.reshape(row_count, features).astype(jnp.bfloat16)
    grad_key = total_k.reshape(row_count, features).astype(jnp.bfloat16)
    grad_value = total_v.reshape(row_count, features).astype(jnp.bfloat16)
    return (output[None], grad_query[None], grad_key[None], grad_value[None], grad_proj)


def solution(mesh):
    in_specs = (
        P("batch", "tm", None),
        P("batch", "tm", None),
        P("batch", "tm", None),
        P(),
        P("batch", "tm", None),
    )
    out_specs = (
        P("batch", "tm", None),
        P("batch", "tm", None),
        P("batch", "tm", None),
        P("batch", "tm", None),
        P(("tm", "batch"), None),
    )
    return jax.shard_map(
        on_device, mesh=mesh, in_specs=in_specs, out_specs=out_specs, check_vma=False
    )
```

```python
import jax
import jax.numpy as jnp
import numpy as np
from jax import lax
from jax.sharding import PartitionSpec as P

HEADS = 8
HD = 64
R2 = 8
R3 = 16


def partner(value, axis, apart):
    mask = 2**apart
    pairs = [(source, source ^ mask) for source in range(lax.axis_size(axis))]
    return lax.ppermute(value, axis, pairs)


def offset_mask(dilation):
    return (np.arange(dilation)[:, None] == (np.arange(HEADS) % dilation)[None, :]).astype(
        np.float32
    )


def cover_table(row_count, dilation):
    return (np.arange(row_count) % dilation)[:, None] == (np.arange(HEADS) % dilation)[None, :]


def pick_rows(matrix, dilation):
    count = matrix.shape[0] // dilation
    blocks = matrix.reshape(count, dilation, HEADS, HD)
    chooser = jnp.asarray(offset_mask(dilation), matrix.dtype)[None, :, :, None]
    return jnp.sum(blocks * chooser, axis=1).reshape(count, HEADS * HD)


def pick_stats(matrix, dilation):
    count = matrix.shape[0] // dilation
    blocks = matrix.reshape(count, dilation, HEADS)
    chooser = jnp.asarray(offset_mask(dilation), matrix.dtype)[None, :, :]
    return jnp.sum(blocks * chooser, axis=1)


def spread_rows(values, dilation):
    chooser = jnp.asarray(offset_mask(dilation), values.dtype)[None, :, :, None]
    return (values[:, None] * chooser).reshape(values.shape[0] * dilation, HEADS, HD)


def spread_stats(values, dilation):
    chooser = jnp.asarray(offset_mask(dilation), values.dtype)[None, :, :]
    return (values[:, None] * chooser).reshape(values.shape[0] * dilation, HEADS)


def merge_levels(log_totals, coverage, partials):
    first_lse = log_totals[0]
    peak = first_lse
    for level_no in range(1, len(log_totals)):
        peak = jnp.maximum(peak, jnp.where(coverage[level_no], log_totals[level_no], first_lse))
    exponents = []
    for level_no in range(len(log_totals)):
        exponents.append(jnp.where(coverage[level_no], jnp.exp(log_totals[level_no] - peak), 0.0))
    denominator = exponents[0]
    for level_no in range(1, len(exponents)):
        denominator = denominator + exponents[level_no]
    weights = []
    merged = None
    for level_no in range(len(exponents)):
        weight_now = exponents[level_no] / denominator
        weights.append(weight_now)
        term = weight_now[:, :, None] * partials[level_no]
        merged = term if merged is None else merged + term
    return (merged, weights)


def gather_blocks(block, axis_pos, bit_order):
    for bit_pos in bit_order:
        block = jnp.concatenate([block, partner(block, "tm", bit_pos)], axis_pos)
    return block


def gather_with_rider(block, axis_pos, bit_order, rider):
    lanes = block.shape[-1]
    for bit_pos in bit_order:
        if bit_pos == 0:
            rows = block.size // lanes
            message = jnp.concatenate([block.reshape(rows, lanes), rider.reshape(-1, lanes)], 0)
            got = partner(message, "tm", bit_pos)
            other = got[:rows].reshape(block.shape)
            rider_back = got[rows:].reshape(rider.shape)
        else:
            other = partner(block, "tm", bit_pos)
        block = jnp.concatenate([block, other], axis_pos)
    return block, rider_back


def split_exact(values):
    high = lax.reduce_precision(values, exponent_bits=8, mantissa_bits=7)
    rest = values - high
    middle = lax.reduce_precision(rest, exponent_bits=8, mantissa_bits=7)
    low = rest - middle
    parts = jnp.concatenate([high, middle, low], -1)
    return parts.astype(jnp.bfloat16)


def join_exact(parts):
    width = parts.shape[-1] // 3
    as32 = parts.astype(jnp.float32)
    return as32[..., :width] + (as32[..., width : 2 * width] + as32[..., 2 * width :])


def by_parity(rows):
    return rows.reshape((rows.shape[0] // 2, 2) + rows.shape[1:]).swapaxes(0, 1)


def from_parity(rows):
    return rows.swapaxes(0, 1).reshape((rows.shape[0] * rows.shape[1],) + rows.shape[2:])


def pad_lanes(matrix, width):
    return jnp.pad(matrix, [(0, 0)] * (matrix.ndim - 1) + [(0, width - matrix.shape[-1])])


def scatter_sum(matrix, axes, bit_order):
    index = lax.axis_index(axes)
    bit_count = len(bit_order)
    size = 1 << bit_count
    block = matrix.reshape((2,) * bit_count + matrix.shape[1:])
    dims = [bit_count - 1 - j for j in range(bit_count)]
    for bit_pos in bit_order[:-2]:
        axis_pos = dims.index(bit_pos)
        my_bit = index // (1 << bit_pos) % 2
        keep = lax.dynamic_index_in_dim(block, my_bit, axis_pos, keepdims=False)
        send = lax.dynamic_index_in_dim(block, 1 - my_bit, axis_pos, keepdims=False)
        pairs = [(source, source ^ (1 << bit_pos)) for source in range(size)]
        block = keep + lax.ppermute(send, axes, pairs)
        dims.pop(axis_pos)
    high_bit, low_bit = dims
    block = block.reshape((4,) + matrix.shape[1:])
    mine = index // (1 << high_bit) % 2 * 2 + index // (1 << low_bit) % 2
    total = lax.dynamic_index_in_dim(block, mine, 0, keepdims=False)
    for flip in range(1, 4):
        mask = (flip // 2 << high_bit) | (flip % 2 << low_bit)
        send = lax.dynamic_index_in_dim(block, mine ^ flip, 0, keepdims=False)
        pairs = [(source, source ^ mask) for source in range(size)]
        total = total + lax.ppermute(send, axes, pairs)
    return total.reshape((1,) + matrix.shape[1:])


def heads_view(matrix):
    return matrix.reshape(matrix.shape[0], HEADS, HD)


def attend(query_rows, key_rows, value_rows, inv_root):
    scores = (
        jnp.einsum(
            "qhd,khd->hqk",
            heads_view(query_rows),
            heads_view(key_rows),
            preferred_element_type=jnp.float32,
        )
        * inv_root
    )
    peak = jnp.max(scores, axis=2, keepdims=True)
    log_total = peak + jnp.log(jnp.sum(jnp.exp(scores - peak), axis=2, keepdims=True))
    weights_bf = jnp.exp(scores - log_total).astype(jnp.bfloat16)
    part_out = jnp.einsum(
        "hqk,khd->qhd", weights_bf, heads_view(value_rows), preferred_element_type=jnp.float32
    )
    return part_out, log_total[:, :, 0].T


def near_grad(query_rows, key_rows, value_rows, grad_rows, lse_rows, offset_rows, inv_root):
    scores = (
        jnp.einsum(
            "qhd,khd->hqk",
            heads_view(query_rows),
            heads_view(key_rows),
            preferred_element_type=jnp.float32,
        )
        * inv_root
    )
    prob_full = jnp.exp(scores - lse_rows.T[:, :, None])
    dprob = jnp.einsum(
        "qhd,khd->hqk",
        heads_view(grad_rows),
        heads_view(value_rows),
        preferred_element_type=jnp.float32,
    )
    dscore = (prob_full * (dprob - offset_rows.T[:, :, None])).astype(jnp.bfloat16)
    return (
        jnp.einsum("hqk,khd->qhd", dscore, heads_view(key_rows), preferred_element_type=jnp.float32)
        * inv_root
    )


def far_grad(query_group, grad_group, lse_group, offset_group, key_rows, value_rows, inv_root):
    scores_far = (
        jnp.einsum(
            "qhd,khd->hqk",
            heads_view(query_group),
            heads_view(key_rows),
            preferred_element_type=jnp.float32,
        )
        * inv_root
    )
    prob_far = jnp.exp(scores_far - lse_group.T[:, :, None])
    grad_v = jnp.einsum(
        "hqk,qhd->khd",
        prob_far.astype(jnp.bfloat16),
        heads_view(grad_group),
        preferred_element_type=jnp.float32,
    )
    dprob_far = jnp.einsum(
        "qhd,khd->hqk",
        heads_view(grad_group),
        heads_view(value_rows),
        preferred_element_type=jnp.float32,
    )
    dscore_far = (prob_far * (dprob_far - offset_group.T[:, :, None])).astype(jnp.bfloat16)
    grad_k = (
        jnp.einsum(
            "hqk,qhd->khd", dscore_far, heads_view(query_group), preferred_element_type=jnp.float32
        )
        * inv_root
    )
    return grad_k, grad_v


def on_device(query_states, key_states, value_states, out_proj, grad_output):
    queries = query_states[0]
    keys_all = key_states[0]
    values_all = value_states[0]
    upstream = grad_output[0]
    row_count = queries.shape[0]
    features = queries.shape[1]
    inv_root = HD ** (-0.5)
    devices = lax.axis_size("tm")
    bit_count = devices.bit_length() - 1
    top_bit = bit_count - 1
    near_first = {0: 3, 1: 1, 2: 0, 3: 4, 4: 2, 5: 5}
    low_bits = sorted(range(top_bit), key=lambda b: near_first.get(b, b))
    wide = features + 128

    qkv = jnp.stack([by_parity(pick_rows(m, R2)) for m in (queries, keys_all, values_all)], 0)
    per_par = qkv.shape[2]
    own, other_qkv = gather_with_rider(
        qkv[:, :, None], 2, low_bits, jnp.stack([queries, keys_all, values_all], 0)
    )
    far = partner(own[:, 0], "tm", top_bit)
    other_q = other_qkv[0]
    keys_one = jnp.concatenate([keys_all, other_qkv[1]], 0)
    values_one = jnp.concatenate([values_all, other_qkv[2]], 0)
    part_one, lse_one = attend(queries, keys_one, values_one, inv_root)
    q_seg2 = own[0].reshape(-1, features)
    k_seg2 = own[1].reshape(-1, features)
    v_seg2 = own[2].reshape(-1, features)
    q_seg3 = jnp.concatenate([own[0, 0], far[0]], 0).reshape(-1, features)
    k_seg3 = jnp.concatenate([own[1, 0], far[1]], 0).reshape(-1, features)
    v_seg3 = jnp.concatenate([own[2, 0], far[2]], 0).reshape(-1, features)
    q_two = qkv[0].reshape(-1, features)
    q_three = qkv[0, 0]
    part_two, lse_two = attend(q_two, k_seg2, v_seg2, inv_root)
    part_three, lse_three = attend(q_three, k_seg3, v_seg3, inv_root)

    partials = [
        spread_rows(part_one, 1),
        spread_rows(from_parity(part_two.reshape((2, per_par) + part_two.shape[1:])), R2),
        spread_rows(part_three, R3),
    ]
    log_totals = [
        spread_stats(lse_one, 1),
        spread_stats(from_parity(lse_two.reshape(2, per_par, HEADS)), R2),
        spread_stats(lse_three, R3),
    ]
    coverage = [cover_table(row_count, d) for d in (1, R2, R3)]
    merged, weights = merge_levels(log_totals, coverage, partials)
    attn = merged.reshape(row_count, features).astype(jnp.bfloat16)
    output = jnp.dot(attn, out_proj, preferred_element_type=jnp.float32).astype(jnp.bfloat16)
    grad_attn = lax.dot_general(
        upstream, out_proj, (((1,), (1,)), ((), ())), preferred_element_type=jnp.float32
    ).astype(jnp.bfloat16)
    proj_part = lax.dot_general(
        attn, upstream, (((0,), (0,)), ((), ())), preferred_element_type=jnp.float32
    )
    order = (0, 2, 5, 7, 3, 6, 8, 4, 1)
    grad_proj = scatter_sum(proj_part, ("tm", "batch"), order)

    grad_three = grad_attn.astype(jnp.float32).reshape(row_count, HEADS, HD)
    rowdot = jnp.sum(grad_three * merged, axis=2)

    def grad_of(weight_now, grad_rows):
        scaled = weight_now[:, :, None] * grad_rows.astype(jnp.float32).reshape(-1, HEADS, HD)
        return scaled.astype(jnp.bfloat16).reshape(-1, features)

    grad_one = grad_of(weights[0], grad_attn)
    offset_one = weights[0] * rowdot
    packed_one = jnp.concatenate([grad_one, split_exact(jnp.concatenate([lse_one, offset_one], 1))], 1)

    ga_par = by_parity(pick_rows(grad_attn, R2))
    w_two = by_parity(pick_stats(weights[1], R2))
    rd_two = by_parity(pick_stats(rowdot, R2))
    lse_two_par = lse_two.reshape(2, per_par, HEADS)
    w_three = pick_stats(weights[2], R3)
    no_level = jnp.zeros_like(w_three)
    lse3_par = jnp.stack([lse_three, no_level], 0)
    w3_par = jnp.stack([w_three, no_level], 0)
    stats_par = jnp.concatenate([lse_two_par, w_two, lse3_par, w3_par, rd_two], -1)
    packed = pad_lanes(jnp.concatenate([ga_par, split_exact(stats_par)], -1), wide)
    own_b, other_one = gather_with_rider(packed[:, None], 1, low_bits, pad_lanes(packed_one, wide))
    other_stats = join_exact(other_one[:, features : features + 6 * HEADS])
    total_q = spread_rows(
        near_grad(queries, keys_one, values_one, grad_one, lse_one, offset_one, inv_root), 1
    )
    k_g1, v_g1 = far_grad(
        jnp.concatenate([queries, other_q], 0),
        jnp.concatenate([grad_one, other_one[:, :features]], 0),
        jnp.concatenate([lse_one, other_stats[:, :HEADS]], 0),
        jnp.concatenate([offset_one, other_stats[:, HEADS:]], 0),
        keys_all,
        values_all,
        inv_root,
    )
    total_k = spread_rows(k_g1, 1)
    total_v = spread_rows(v_g1, 1)
    far_b = partner(own_b[0], "tm", top_bit)
    stat_w = 5 * HEADS

    def unpack(rows):
        rows = rows.reshape(-1, wide)
        stats = join_exact(rows[:, features : features + 3 * stat_w])
        return rows[:, :features], stats.reshape(-1, 5, HEADS)

    g_two = grad_of(w_two.reshape(-1, HEADS), ga_par.reshape(-1, features))
    c_two = w_two.reshape(-1, HEADS) * rd_two.reshape(-1, HEADS)
    grad_q2 = near_grad(q_two, k_seg2, v_seg2, g_two, lse_two, c_two, inv_root)
    ga_seg2, st_seg2 = unpack(own_b)
    k_g2, v_g2 = far_grad(
        q_seg2,
        grad_of(st_seg2[:, 1], ga_seg2),
        st_seg2[:, 0],
        st_seg2[:, 1] * st_seg2[:, 4],
        qkv[1].reshape(-1, features),
        qkv[2].reshape(-1, features),
        inv_root,
    )

    g_three = grad_of(w_three, ga_par[0])
    c_three = w_three * rd_two[0]
    grad_q3 = near_grad(q_three, k_seg3, v_seg3, g_three, lse_three, c_three, inv_root)
    ga_seg3, st_seg3 = unpack(jnp.concatenate([own_b[0], far_b], 0))
    k_g3, v_g3 = far_grad(
        q_seg3,
        grad_of(st_seg3[:, 3], ga_seg3),
        st_seg3[:, 2],
        st_seg3[:, 3] * st_seg3[:, 4],
        qkv[1, 0],
        qkv[2, 0],
        inv_root,
    )

    def level_two_rows(values):
        return spread_rows(from_parity(values.reshape((2, per_par) + values.shape[1:])), R2)

    total_q = total_q + level_two_rows(grad_q2) + spread_rows(grad_q3, R3)
    total_k = total_k + level_two_rows(k_g2) + spread_rows(k_g3, R3)
    total_v = total_v + level_two_rows(v_g2) + spread_rows(v_g3, R3)
    grad_query = total_q.reshape(row_count, features).astype(jnp.bfloat16)
    grad_key = total_k.reshape(row_count, features).astype(jnp.bfloat16)
    grad_value = total_v.reshape(row_count, features).astype(jnp.bfloat16)
    return (output[None], grad_query[None], grad_key[None], grad_value[None], grad_proj)


def solution(mesh):
    in_specs = (
        P("batch", "tm", None),
        P("batch", "tm", None),
        P("batch", "tm", None),
        P(),
        P("batch", "tm", None),
    )
    out_specs = (
        P("batch", "tm", None),
        P("batch", "tm", None),
        P("batch", "tm", None),
        P("batch", "tm", None),
        P(("tm", "batch"), None),
    )
    return jax.shard_map(
        on_device, mesh=mesh, in_specs=in_specs, out_specs=out_specs, check_vma=False
    )
```
